128 devices in a mesh: dp: 8 (over z, y_lo), slab: 16 (over y_hi, x, core).
Axes of the slice: x: 4, y: 4 (y_hi: 2, y_lo: 2; y = y_hi * 2 + y_lo), z: 4, core: 2. Of those that a mesh axis runs over, the one named last changes fastest.
Arguments:
- sensitivity: bfloat16 [8192, 128, 256], P('dp', 'slab'), may hold values from -6 to 6
- cell_class: int32 [128, 256], P('slab'), may hold values from 0 to 7
- class_rate: float32 [8], replicated, may hold values from 0.28 to 0.4
- panel_owner: int32 [8], replicated, may hold values from 0 to 7, each once
Outputs:
- smoothed: float32 [8192, 128, 256], P('dp', 'slab')
- gram: float32 [8192, 3, 256], P(('dp', 'slab'))
The draws below stay inside these ranges and needn't reach their ends.
Inputs may be any that keep to these rules, and one draw needn't show every extreme that they name: `panel_owner`: each dp index appears exactly once.
All inputs are finite; a program needn't handle non-finite values.
Results may differ from the reference program's by a relative error of at most 0.002.
Values may be sent and summed in bfloat16 or wider, within the bound.
No kernel may reach another device: no remote copies, remote signals or barrier semaphores. Data moves between devices by JAX's collectives and lax.ppermute only.
A program may use at most 128 MiB of HBM per device.

```python
import math
import jax
import jax.numpy as jnp
from jax import lax

ROWS_DEV = 1024
LX = 16
PASSES = 4
PANELS = 3
PANEL = 256
CLASSES = 8
LAT = 256
DATA = 8192
NZ = 128
N_DP = 8


def set_ends(array, rng, least, top_value):
    place = [jax.random.randint(jax.random.fold_in(rng, axis), (), 0, length) for axis, length in enumerate(array.shape)]
    longest = array.shape.index(max(array.shape))
    beside = place[:longest] + [(place[longest] + 1) % array.shape[longest]] + place[longest + 1:]
    return array.at[tuple(place)].set(least).at[tuple(beside)].set(top_value)


def levels(rng, shape, pieces, least, high):
    def one(axis_at, blocks):
        draws = jax.random.uniform(jax.random.fold_in(jax.random.fold_in(rng, 6), axis_at), (blocks,), jnp.float32, least / len(pieces), high / len(pieces))
        return jnp.repeat(jnp.exp(draws), shape[axis_at] // blocks).reshape((-1,) + (1,) * (len(shape) - axis_at - 1))

    gain = one(*pieces[0])
    for cut in pieces[1:]:
        gain = gain * one(*cut)
    return gain


def normal_values(own_key, shape, scale, limit, split=(), held_as=jnp.bfloat16):
    entries = scale * jax.random.normal(own_key, shape, jnp.float32)
    if split:
        entries = entries * levels(own_key, shape, split, -0.22, 0.18)
    return jnp.clip(entries, -limit, limit).astype(held_as)


def setup_inputs(seed: int = 0) -> dict:
    streams_of = jax.random.split(jax.random.key(seed), 5)
    return {
        "sensitivity": normal_values(streams_of[0], (DATA, NZ, LAT), 1.0, 6.0, ((0, 8), (1, 16))),
        "cell_class": set_ends(jax.random.randint(streams_of[1], (NZ, LAT), 0, CLASSES), jax.random.fold_in(streams_of[1], 1), 0, CLASSES - 1).astype(jnp.int32),
        "class_rate": jnp.clip(jnp.exp(jax.random.uniform(streams_of[2], (CLASSES,), jnp.float32, math.log(0.28), math.log(0.4))), 0.28, 0.4),
        "panel_owner": jax.random.permutation(streams_of[3], N_DP).astype(jnp.int32),
    }


lateral_weight = 0.125


def shift_last(v, s):
    zeros = jnp.zeros(v.shape[:-1] + (abs(s),), v.dtype)
    if s > 0:
        return jnp.concatenate([zeros, v[..., :-s]], axis=-1)
    return jnp.concatenate([v[..., -s:], zeros], axis=-1)


def lateral_sum(v, side):
    column = jnp.arange(v.shape[-1]) % side
    low_mask = (column != 0).astype(jnp.float32)
    high_mask = (column != side - 1).astype(jnp.float32)
    total = shift_last(v, side) + shift_last(v, -side)
    return total + low_mask * shift_last(v, 1) + high_mask * shift_last(v, -1)


def smooth_block(block, kappa):
    v = block.astype(jnp.float32)
    for step in range(PASSES):
        padded = jnp.pad(v, ((0, 0), (1, 1), (0, 0)))
        depth_sum = padded[:, 2:] + padded[:, :-2]
        v = v + kappa * (depth_sum - 2.0 * v) + (lateral_weight * kappa) * (lateral_sum(v, LX) - 4.0 * v)
    return v


def reference(sensitivity, cell_class, class_rate, panel_owner):
    kappa = class_rate[cell_class]
    blocks = sensitivity.reshape(N_DP, ROWS_DEV, NZ, LAT)
    smoothed = lax.map(lambda b: smooth_block(b, kappa), blocks)
    panels = []
    for p in range(PANELS):
        owned = lax.dynamic_index_in_dim(smoothed, panel_owner[p].astype(jnp.int32), 0, keepdims=False)
        panels.append(owned[p * PANEL:(p + 1) * PANEL].reshape(PANEL, NZ * LAT).astype(jnp.bfloat16))
    stacked = jnp.concatenate(panels, axis=0)

    def block_gram(b):
        flat = b.reshape(ROWS_DEV, NZ * LAT)
        return lax.dot_general(flat, stacked, (((1,), (1,)), ((), ())), preferred_element_type=jnp.float32)

    gram = lax.map(block_gram, blocks) / (NZ * LAT)
    return smoothed.reshape(DATA, NZ, LAT), gram.reshape(DATA, PANELS, PANEL)
```

```python
import functools

import jax
import jax.numpy as jnp
from jax import lax
from jax.experimental import pallas as pl
from jax.experimental.pallas import tpu as pltpu
from jax.sharding import PartitionSpec as P

LX = 16
PASSES = 4
PANELS = 3
PANEL = 256
HALO = 4

lateral_weight = 0.125


def from_root(value, axis, source):
    kept = jnp.where(lax.axis_index(axis) == source, value, 0).astype(value.dtype)
    return lax.psum(kept, axis)


def halo_of(shard, axis, dim):
    size, length = lax.axis_size(axis), shard.shape[dim]
    up = [(i, i + 1) for i in range(size - 1)]
    down = [(j, i) for i, j in up]
    top = lax.slice_in_dim(shard, length - HALO, length, axis=dim)
    bottom = lax.slice_in_dim(shard, 0, HALO, axis=dim)
    below = lax.ppermute(top, axis, up)
    above = lax.ppermute(bottom, axis, down)
    return jnp.concatenate([below, above], axis=dim)


def smooth_kernel(ka_ref, kb_ref, a_ref, b_ref, o_ref, *, sub):
    depth, lat = ka_ref.shape
    shape = (sub, depth, lat)
    lane = lax.broadcasted_iota(jnp.int32, shape, 2)
    row = lax.broadcasted_iota(jnp.int32, shape, 1)
    col = lane % LX
    ka = jnp.broadcast_to(ka_ref[...][None], shape)
    kb = jnp.broadcast_to(kb_ref[...][None], shape)

    def coeffs(k):
        k8 = lateral_weight * k
        return (
            k,
            1.0 - 2.0 * k - 4.0 * k8,
            jnp.where(lane >= LX, k8, 0.0),
            jnp.where(lane < lat - LX, k8, 0.0),
            jnp.where(col != 0, k8, 0.0),
            jnp.where(col != LX - 1, k8, 0.0),
        )

    ca, cb = coeffs(ka), coeffs(kb)
    first_a, last_a = row == 0, row == depth - 1
    first_b, last_b = row == HALO, row == HALO - 1

    def step(v, down, up, c):
        k, cself, c_xm, c_xp, c_ym, c_yp = c
        lateral = (
            c_xm * pltpu.roll(v, LX, 2)
            + c_xp * pltpu.roll(v, lat - LX, 2)
            + c_ym * pltpu.roll(v, 1, 2)
            + c_yp * pltpu.roll(v, lat - 1, 2)
        )
        return cself * v + k * (down + up) + lateral

    def body(i, carry):
        r = pl.multiple_of(i * sub, sub)
        a = a_ref[pl.ds(r, sub)].astype(jnp.float32)
        b = b_ref[pl.ds(r, sub)].astype(jnp.float32)
        for _ in range(PASSES):
            a_dn = jnp.where(first_a, pltpu.roll(b, depth - HALO + 1, 1), pltpu.roll(a, 1, 1))
            a_up = jnp.where(last_a, pltpu.roll(b, HALO - 1, 1), pltpu.roll(a, depth - 1, 1))
            b_dn = jnp.where(first_b, pltpu.roll(a, depth - HALO + 1, 1), pltpu.roll(b, 1, 1))
            b_up = jnp.where(last_b, pltpu.roll(a, HALO - 1, 1), pltpu.roll(b, depth - 1, 1))
            a, b = step(a, a_dn, a_up, ca), step(b, b_dn, b_up, cb)
        o_ref[pl.ds(r, sub)] = a
        return carry

    lax.fori_loop(0, a_ref.shape[0] // sub, body, 0)


def smooth(sensitivity, halo, kappa, kappa_halo, block=128, sub=2):
    rows, depth, lat = sensitivity.shape
    kernel = functools.partial(smooth_kernel, sub=sub)
    return pl.pallas_call(
        kernel,
        grid=(rows // block,),
        in_specs=[
            pl.BlockSpec((depth, lat), lambda i: (0, 0)),
            pl.BlockSpec((depth, lat), lambda i: (0, 0)),
            pl.BlockSpec((block, depth, lat), lambda i: (i, 0, 0)),
            pl.BlockSpec((block, depth, lat), lambda i: (i, 0, 0)),
        ],
        out_specs=pl.BlockSpec((block, depth, lat), lambda i: (i, 0, 0)),
        out_shape=jax.ShapeDtypeStruct((rows, depth, lat), jnp.float32),
    )(kappa, kappa_halo, sensitivity, halo)


def body(sensitivity, cell_class, class_rate, panel_owner):
    rows, depth, lat = sensitivity.shape
    onehot = (cell_class[..., None] == jnp.arange(class_rate.shape[0])[None, None, :]).astype(
        jnp.float32
    )
    kappa = jnp.sum(onehot * class_rate[None, None, :], axis=-1)
    halo = halo_of(sensitivity, "slab", 1)
    kappa_halo = halo_of(kappa, "slab", 0)
    field = smooth(sensitivity, halo, kappa, kappa_halo)
    cells = depth * lat * lax.axis_size("slab")
    flat = sensitivity.reshape(rows, depth * lat)
    partials = []
    for p in range(PANELS):
        piece = field[p * PANEL : (p + 1) * PANEL].reshape(PANEL, depth * lat).astype(jnp.bfloat16)
        received = from_root(piece, "dp", panel_owner[p])
        term = (
            lax.dot_general(
                flat, received, (((1,), (1,)), ((), ())), preferred_element_type=jnp.float32
            )
            / cells
        )
        partials.append(lax.psum_scatter(term, "slab", scatter_dimension=0, tiled=True))
    gram = jnp.stack(partials, axis=1)
    return (field, gram)


def solution(mesh):
    placed = (P("dp", "slab", None), P("slab", None), P(), P())
    return jax.shard_map(
        body,
        mesh=mesh,
        in_specs=placed,
        out_specs=(P("dp", "slab", None), P(("dp", "slab"), None, None)),
        check_vma=False,
    )
```

```python
import functools

import jax
import jax.numpy as jnp
from jax import lax
from jax.experimental import pallas as pl
from jax.experimental.pallas import tpu as pltpu
from jax.sharding import PartitionSpec as P

LX = 16
PASSES = 4
PANELS = 3
PANEL = 256
HALO = 4

lateral_weight = 0.125


def broadcast_dp(piece, owner, axis):
    size = lax.axis_size(axis)
    me = lax.axis_index(axis)
    ring = size // 2
    z, oz = me // 2, owner // 2
    pair = lax.ppermute(piece, axis, [(i, i ^ 1) for i in range(size)])
    val = jnp.where(me == owner, piece, pair)
    from_below = lax.ppermute(val, axis, [(i, (i + 2) % size) for i in range(size)])
    from_above = lax.ppermute(val, axis, [(i, (i - 2) % size) for i in range(size)])
    val = jnp.where(z == oz, val, jnp.where(z == (oz + 1) % ring, from_below, from_above))
    last = lax.ppermute(val, axis, [(i, (i + 2) % size) for i in range(size)])
    return jnp.where(z == (oz + 2) % ring, last, val)


def reduce_scatter_slab(term, axis):
    size = lax.axis_size(axis)
    me = lax.axis_index(axis)
    rows = term.shape[0] // size
    part = term.reshape((size, rows) + term.shape[1:])
    bit = 1
    while bit < size:
        mine = (me // bit) % 2
        halves = part.reshape((part.shape[0] // 2, 2) + part.shape[1:])
        keep = lax.dynamic_index_in_dim(halves, mine, axis=1, keepdims=False)
        send = lax.dynamic_index_in_dim(halves, 1 - mine, axis=1, keepdims=False)
        part = keep + lax.ppermute(send, axis, [(i, i ^ bit) for i in range(size)])
        bit *= 2
    return part.reshape((rows,) + term.shape[1:])


def halo_of(shard, axis, dim):
    size, length = lax.axis_size(axis), shard.shape[dim]
    up = [(i, i + 1) for i in range(size - 1)]
    down = [(j, i) for i, j in up]
    top = lax.slice_in_dim(shard, length - HALO, length, axis=dim)
    bottom = lax.slice_in_dim(shard, 0, HALO, axis=dim)
    below = lax.ppermute(top, axis, up)
    above = lax.ppermute(bottom, axis, down)
    return jnp.concatenate([below, above], axis=dim)


def smooth_kernel(ka_ref, kb_ref, a_ref, b_ref, o_ref, *, sub):
    depth, lat = ka_ref.shape
    shape = (sub, depth, lat)
    lane = lax.broadcasted_iota(jnp.int32, shape, 2)
    row = lax.broadcasted_iota(jnp.int32, shape, 1)
    col = lane % LX
    ka = jnp.broadcast_to(ka_ref[...][None], shape)
    kb = jnp.broadcast_to(kb_ref[...][None], shape)

    def coeffs(k):
        k8 = lateral_weight * k
        return (
            k,
            1.0 - 2.0 * k - 4.0 * k8,
            jnp.where(lane >= LX, k8, 0.0),
            jnp.where(lane < lat - LX, k8, 0.0),
            jnp.where(col != 0, k8, 0.0),
            jnp.where(col != LX - 1, k8, 0.0),
        )

    ca, cb = coeffs(ka), coeffs(kb)
    first_a, last_a = row == 0, row == depth - 1
    first_b, last_b = row == HALO, row == HALO - 1

    def step(v, down, up, c):
        k, cself, c_xm, c_xp, c_ym, c_yp = c
        lateral = (
            c_xm * pltpu.roll(v, LX, 2)
            + c_xp * pltpu.roll(v, lat - LX, 2)
            + c_ym * pltpu.roll(v, 1, 2)
            + c_yp * pltpu.roll(v, lat - 1, 2)
        )
        return cself * v + k * (down + up) + lateral

    def body(i, carry):
        r = pl.multiple_of(i * sub, sub)
        a = a_ref[pl.ds(r, sub)].astype(jnp.float32)
        b = b_ref[pl.ds(r, sub)].astype(jnp.float32)
        for _ in range(PASSES):
            a_dn = jnp.where(first_a, pltpu.roll(b, depth - HALO + 1, 1), pltpu.roll(a, 1, 1))
            a_up = jnp.where(last_a, pltpu.roll(b, HALO - 1, 1), pltpu.roll(a, depth - 1, 1))
            b_dn = jnp.where(first_b, pltpu.roll(a, depth - HALO + 1, 1), pltpu.roll(b, 1, 1))
            b_up = jnp.where(last_b, pltpu.roll(a, HALO - 1, 1), pltpu.roll(b, depth - 1, 1))
            a, b = step(a, a_dn, a_up, ca), step(b, b_dn, b_up, cb)
        o_ref[pl.ds(r, sub)] = a
        return carry

    lax.fori_loop(0, a_ref.shape[0] // sub, body, 0)


def smooth(sensitivity, halo, kappa, kappa_halo, block=128, sub=2):
    rows, depth, lat = sensitivity.shape
    kernel = functools.partial(smooth_kernel, sub=sub)
    return pl.pallas_call(
        kernel,
        grid=(rows // block,),
        in_specs=[
            pl.BlockSpec((depth, lat), lambda i: (0, 0)),
            pl.BlockSpec((depth, lat), lambda i: (0, 0)),
            pl.BlockSpec((block, depth, lat), lambda i: (i, 0, 0)),
            pl.BlockSpec((block, depth, lat), lambda i: (i, 0, 0)),
        ],
        out_specs=pl.BlockSpec((block, depth, lat), lambda i: (i, 0, 0)),
        out_shape=jax.ShapeDtypeStruct((rows, depth, lat), jnp.float32),
    )(kappa, kappa_halo, sensitivity, halo)


def body(sensitivity, cell_class, class_rate, panel_owner):
    rows, depth, lat = sensitivity.shape
    onehot = (cell_class[..., None] == jnp.arange(class_rate.shape[0])[None, None, :]).astype(
        jnp.float32
    )
    kappa = jnp.sum(onehot * class_rate[None, None, :], axis=-1)
    halo = halo_of(sensitivity, "slab", 1)
    kappa_halo = halo_of(kappa, "slab", 0)
    field = smooth(sensitivity, halo, kappa, kappa_halo)
    cells = depth * lat * lax.axis_size("slab")
    flat = sensitivity.reshape(rows, depth * lat)
    partials = []
    for p in range(PANELS):
        piece = field[p * PANEL : (p + 1) * PANEL].reshape(PANEL, depth * lat).astype(jnp.bfloat16)
        received = broadcast_dp(piece, panel_owner[p], "dp")
        term = (
            lax.dot_general(
                flat, received, (((1,), (1,)), ((), ())), preferred_element_type=jnp.float32
            )
            / cells
        )
        partials.append(reduce_scatter_slab(term, "slab"))
    gram = jnp.stack(partials, axis=1)
    return (field, gram)


def solution(mesh):
    placed = (P("dp", "slab", None), P("slab", None), P(), P())
    return jax.shard_map(
        body,
        mesh=mesh,
        in_specs=placed,
        out_specs=(P("dp", "slab", None), P(("dp", "slab"), None, None)),
        check_vma=False,
    )
```

```python
import functools

import jax
import jax.numpy as jnp
from jax import lax
from jax.experimental import pallas as pl
from jax.experimental.pallas import tpu as pltpu
from jax.sharding import PartitionSpec as P

LX = 16
PASSES = 4
PANELS = 3
PANEL = 256
HALO = 4

lateral_weight = 0.125


def broadcast_dp(piece, owner, axis):
    size = lax.axis_size(axis)
    me = lax.axis_index(axis)
    ring = size // 2
    z, oz = me // 2, owner // 2
    pair = lax.ppermute(piece, axis, [(i, i ^ 1) for i in range(size)])
    val = jnp.where(me == owner, piece, pair)
    from_below = lax.ppermute(val, axis, [(i, (i + 2) % size) for i in range(size)])
    from_above = lax.ppermute(val, axis, [(i, (i - 2) % size) for i in range(size)])
    val = jnp.where(z == oz, val, jnp.where(z == (oz + 1) % ring, from_below, from_above))
    last = lax.ppermute(val, axis, [(i, (i + 2) % size) for i in range(size)])
    return jnp.where(z == (oz + 2) % ring, last, val)


def reduce_scatter_slab(term, axis):
    size = lax.axis_size(axis)
    me = lax.axis_index(axis)
    rows = term.shape[0] // size
    part = term.reshape((size, rows) + term.shape[1:])
    bit = 1
    while bit < size:
        mine = (me // bit) % 2
        halves = part.reshape((part.shape[0] // 2, 2) + part.shape[1:])
        keep = lax.dynamic_index_in_dim(halves, mine, axis=1, keepdims=False)
        send = lax.dynamic_index_in_dim(halves, 1 - mine, axis=1, keepdims=False)
        part = keep + lax.ppermute(send, axis, [(i, i ^ bit) for i in range(size)])
        bit *= 2
    return part.reshape((rows,) + term.shape[1:])


def halo_of(shard, axis, dim):
    size, length = lax.axis_size(axis), shard.shape[dim]
    up = [(i, i + 1) for i in range(size - 1)]
    down = [(j, i) for i, j in up]
    top = lax.slice_in_dim(shard, length - HALO, length, axis=dim)
    bottom = lax.slice_in_dim(shard, 0, HALO, axis=dim)
    below = lax.ppermute(top, axis, up)
    above = lax.ppermute(bottom, axis, down)
    return jnp.concatenate([below, above], axis=dim)


def smooth_kernel(coef_ref, a_ref, h_ref, o_ref, *, sub):
    depth, lat = a_ref.shape[1], a_ref.shape[2]
    half = lat // 2
    shape = (sub, depth, half)
    row = lax.broadcasted_iota(jnp.int32, shape, 1)
    lane = lax.broadcasted_iota(jnp.int32, shape, 2)
    low_rows, first, last = row < HALO, row == 0, row == depth - 1
    low_lanes, high_lanes = lane < LX, lane >= half - LX

    def coef(n, j, h):
        return coef_ref[n, j * depth : (j + 1) * depth, h * half : (h + 1) * half][None]

    def body(i, carry):
        r = pl.multiple_of(i * sub, sub)
        own = a_ref[pl.ds(r, sub)].astype(jnp.float32)
        hal = h_ref[pl.ds(r, sub)].astype(jnp.float32)
        own = [own[..., :half], own[..., half:]]
        hal = [hal[..., :half], hal[..., half:]]
        rot = [pltpu.roll(o, HALO, 1) for o in own]
        x = [
            [jnp.where(low_rows, hal[h], rot[h]) for h in range(2)],
            [jnp.where(low_rows, rot[h], hal[h]) for h in range(2)],
        ]
        cf = [[[coef(n, j, h) for h in range(2)] for j in range(2)] for n in range(6)]
        for _ in range(PASSES):
            depth_sum = [[None, None], [None, None]]
            for h in range(2):
                d0, d1 = pltpu.roll(x[0][h], 1, 1), pltpu.roll(x[1][h], 1, 1)
                u0, u1 = pltpu.roll(x[0][h], depth - 1, 1), pltpu.roll(x[1][h], depth - 1, 1)
                depth_sum[0][h] = d0 + jnp.where(last, u1, u0)
                depth_sum[1][h] = jnp.where(first, d0, d1) + u1
            new = [[None, None], [None, None]]
            for j in range(2):
                a, b = x[j]
                ra, rb = pltpu.roll(a, LX, 2), pltpu.roll(b, LX, 2)
                sa, sb = pltpu.roll(a, half - LX, 2), pltpu.roll(b, half - LX, 2)
                xm = [ra, jnp.where(low_lanes, ra, rb)]
                xp = [jnp.where(high_lanes, sb, sa), sb]
                for h, v in enumerate((a, b)):
                    k, cself, c_xm, c_xp, c_ym, c_yp = (cf[n][j][h] for n in range(6))
                    lateral = (
                        c_xm * xm[h]
                        + c_xp * xp[h]
                        + c_ym * pltpu.roll(v, 1, 2)
                        + c_yp * pltpu.roll(v, half - 1, 2)
                    )
                    new[j][h] = cself * v + k * depth_sum[j][h] + lateral
            x = new
        for h in range(2):
            out = jnp.where(low_rows, pltpu.roll(x[0][h], HALO, 1), pltpu.roll(x[1][h], HALO, 1))
            o_ref[pl.ds(r, sub), :, h * half : (h + 1) * half] = out
        return carry

    lax.fori_loop(0, a_ref.shape[0] // sub, body, 0)


def coefficients(kappa_col, lat):
    lane = jnp.arange(lat)[None, :]
    col = lane % LX
    k8 = lateral_weight * kappa_col
    zero = jnp.zeros_like(kappa_col)
    return jnp.stack(
        [
            kappa_col,
            1.0 - 2.0 * kappa_col - 4.0 * k8,
            jnp.where(lane >= LX, k8, zero),
            jnp.where(lane < lat - LX, k8, zero),
            jnp.where(col != 0, k8, zero),
            jnp.where(col != LX - 1, k8, zero),
        ]
    )


def smooth(sensitivity, halo, coef, block=128, sub=1):
    rows, depth, lat = sensitivity.shape
    kernel = functools.partial(smooth_kernel, sub=sub)
    return pl.pallas_call(
        kernel,
        grid=(rows // block,),
        in_specs=[
            pl.BlockSpec(coef.shape, lambda i: (0, 0, 0)),
            pl.BlockSpec((block, depth, lat), lambda i: (i, 0, 0)),
            pl.BlockSpec((block, depth, lat), lambda i: (i, 0, 0)),
        ],
        out_specs=pl.BlockSpec((block, depth, lat), lambda i: (i, 0, 0)),
        out_shape=jax.ShapeDtypeStruct((rows, depth, lat), jnp.float32),
    )(coef, sensitivity, halo)


def body(sensitivity, cell_class, class_rate, panel_owner):
    rows, depth, lat = sensitivity.shape
    onehot = (cell_class[..., None] == jnp.arange(class_rate.shape[0])[None, None, :]).astype(
        jnp.float32
    )
    kappa = jnp.sum(onehot * class_rate[None, None, :], axis=-1)
    halo = halo_of(sensitivity, "slab", 1)
    kappa_halo = halo_of(kappa, "slab", 0)
    kappa_col = jnp.concatenate([kappa_halo[:HALO], kappa, kappa_halo[HALO:]], axis=0)
    field = smooth(sensitivity, halo, coefficients(kappa_col, lat))
    cells = depth * lat * lax.axis_size("slab")
    flat = sensitivity.reshape(rows, depth * lat)
    partials = []
    for p in range(PANELS):
        piece = field[p * PANEL : (p + 1) * PANEL].reshape(PANEL, depth * lat).astype(jnp.bfloat16)
        received = broadcast_dp(piece, panel_owner[p], "dp")
        term = (
            lax.dot_general(
                flat, received, (((1,), (1,)), ((), ())), preferred_element_type=jnp.float32
            )
            / cells
        )
        partials.append(reduce_scatter_slab(term, "slab"))
    gram = jnp.stack(partials, axis=1)
    return (field, gram)


def solution(mesh):
    placed = (P("dp", "slab", None), P("slab", None), P(), P())
    return jax.shard_map(
        body,
        mesh=mesh,
        in_specs=placed,
        out_specs=(P("dp", "slab", None), P(("dp", "slab"), None, None)),
        check_vma=False,
    )
```

```python
import functools

import jax
import jax.numpy as jnp
from jax import lax
from jax.experimental import pallas as pl
from jax.experimental.pallas import tpu as pltpu
from jax.sharding import PartitionSpec as P

LX = 16
PASSES = 4
PANELS = 3
PANEL = 256
HALO = 4

lateral_weight = 0.125


def broadcast_dp(piece, owner, axis):
    size = lax.axis_size(axis)
    me = lax.axis_index(axis)
    ring = size // 2
    z, oz = me // 2, owner // 2
    pair = lax.ppermute(piece, axis, [(i, i ^ 1) for i in range(size)])
    val = jnp.where(me == owner, piece, pair)
    from_below = lax.ppermute(val, axis, [(i, (i + 2) % size) for i in range(size)])
    from_above = lax.ppermute(val, axis, [(i, (i - 2) % size) for i in range(size)])
    val = jnp.where(z == oz, val, jnp.where(z == (oz + 1) % ring, from_below, from_above))
    last = lax.ppermute(val, axis, [(i, (i + 2) % size) for i in range(size)])
    return jnp.where(z == (oz + 2) % ring, last, val)


def reduce_scatter_slab(term, axis):
    size = lax.axis_size(axis)
    me = lax.axis_index(axis)
    rows = term.shape[0] // size
    part = term.reshape((size, rows) + term.shape[1:])
    bit = 1
    while bit < size:
        mine = (me // bit) % 2
        halves = part.reshape((part.shape[0] // 2, 2) + part.shape[1:])
        keep = lax.dynamic_index_in_dim(halves, mine, axis=1, keepdims=False)
        send = lax.dynamic_index_in_dim(halves, 1 - mine, axis=1, keepdims=False)
        part = keep + lax.ppermute(send, axis, [(i, i ^ bit) for i in range(size)])
        bit *= 2
    return part.reshape((rows,) + term.shape[1:])


def halo_of(shard, axis, dim):
    size, length = lax.axis_size(axis), shard.shape[dim]
    up = [(i, i + 1) for i in range(size - 1)]
    down = [(j, i) for i, j in up]
    top = lax.slice_in_dim(shard, length - HALO, length, axis=dim)
    bottom = lax.slice_in_dim(shard, 0, HALO, axis=dim)
    below = lax.ppermute(top, axis, up)
    above = lax.ppermute(bottom, axis, down)
    return jnp.concatenate([below, above], axis=dim)


def smooth_kernel(coef_ref, a_ref, h_ref, o_ref, *, sub):
    depth, lat = a_ref.shape[1], a_ref.shape[2]
    half = lat // 2
    shape = (sub, depth, half)
    row = lax.broadcasted_iota(jnp.int32, shape, 1)
    lane = lax.broadcasted_iota(jnp.int32, shape, 2)
    low_rows, first, last = row < HALO, row == 0, row == depth - 1
    low_lanes, high_lanes = lane < LX, lane >= half - LX

    def coef(n, j, h):
        return coef_ref[n, j * depth : (j + 1) * depth, h * half : (h + 1) * half][None]

    def body(i, carry):
        r = pl.multiple_of(i * sub, sub)
        own = a_ref[pl.ds(r, sub)].astype(jnp.float32)
        hal = h_ref[pl.ds(r, sub)].astype(jnp.float32)
        own = [own[..., :half], own[..., half:]]
        hal = [hal[..., :half], hal[..., half:]]
        rot = [pltpu.roll(o, HALO, 1) for o in own]
        x = [
            [jnp.where(low_rows, hal[h], rot[h]) for h in range(2)],
            [jnp.where(low_rows, rot[h], hal[h]) for h in range(2)],
        ]
        cf = [[[coef(n, j, h) for h in range(2)] for j in range(2)] for n in range(6)]
        for _ in range(PASSES):
            depth_sum = [[None, None], [None, None]]
            for h in range(2):
                d0, d1 = pltpu.roll(x[0][h], 1, 1), pltpu.roll(x[1][h], 1, 1)
                u0, u1 = pltpu.roll(x[0][h], depth - 1, 1), pltpu.roll(x[1][h], depth - 1, 1)
                depth_sum[0][h] = d0 + jnp.where(last, u1, u0)
                depth_sum[1][h] = jnp.where(first, d0, d1) + u1
            new = [[None, None], [None, None]]
            for j in range(2):
                a, b = x[j]
                ra, rb = pltpu.roll(a, LX, 2), pltpu.roll(b, LX, 2)
                sa, sb = pltpu.roll(a, half - LX, 2), pltpu.roll(b, half - LX, 2)
                xm = [ra, jnp.where(low_lanes, ra, rb)]
                xp = [jnp.where(high_lanes, sb, sa), sb]
                for h, v in enumerate((a, b)):
                    k, cself, c_xm, c_xp, c_ym, c_yp = (cf[n][j][h] for n in range(6))
                    lateral = (
                        c_xm * xm[h]
                        + c_xp * xp[h]
                        + c_ym * pltpu.roll(v, 1, 2)
                        + c_yp * pltpu.roll(v, half - 1, 2)
                    )
                    new[j][h] = cself * v + k * depth_sum[j][h] + lateral
            x = new
        for h in range(2):
            out = jnp.where(low_rows, pltpu.roll(x[0][h], HALO, 1), pltpu.roll(x[1][h], HALO, 1))
            o_ref[pl.ds(r, sub), :, h * half : (h + 1) * half] = out
        return carry

    lax.fori_loop(0, a_ref.shape[0] // sub, body, 0)


def coefficients(kappa_col, lat):
    lane = jnp.arange(lat)[None, :]
    col = lane % LX
    k8 = lateral_weight * kappa_col
    zero = jnp.zeros_like(kappa_col)
    return jnp.stack(
        [
            kappa_col,
            1.0 - 2.0 * kappa_col - 4.0 * k8,
            jnp.where(lane >= LX, k8, zero),
            jnp.where(lane < lat - LX, k8, zero),
            jnp.where(col != 0, k8, zero),
            jnp.where(col != LX - 1, k8, zero),
        ]
    )


def smooth(sensitivity, halo, coef, block=128, sub=16):
    rows, depth, lat = sensitivity.shape
    kernel = functools.partial(smooth_kernel, sub=sub)
    return pl.pallas_call(
        kernel,
        grid=(rows // block,),
        in_specs=[
            pl.BlockSpec(coef.shape, lambda i: (0, 0, 0)),
            pl.BlockSpec((block, depth, lat), lambda i: (i, 0, 0)),
            pl.BlockSpec((block, depth, lat), lambda i: (i, 0, 0)),
        ],
        out_specs=pl.BlockSpec((block, depth, lat), lambda i: (i, 0, 0)),
        out_shape=jax.ShapeDtypeStruct((rows, depth, lat), jnp.float32),
    )(coef, sensitivity, halo)


def body(sensitivity, cell_class, class_rate, panel_owner):
    rows, depth, lat = sensitivity.shape
    onehot = (cell_class[..., None] == jnp.arange(class_rate.shape[0])[None, None, :]).astype(
        jnp.float32
    )
    kappa = jnp.sum(onehot * class_rate[None, None, :], axis=-1)
    halo = halo_of(sensitivity, "slab", 1)
    kappa_halo = halo_of(kappa, "slab", 0)
    kappa_col = jnp.concatenate([kappa_halo[:HALO], kappa, kappa_halo[HALO:]], axis=0)
    field = smooth(sensitivity, halo, coefficients(kappa_col, lat))
    cells = depth * lat * lax.axis_size("slab")
    flat = sensitivity.reshape(rows, depth * lat)
    partials = []
    for p in range(PANELS):
        piece = field[p * PANEL : (p + 1) * PANEL].reshape(PANEL, depth * lat).astype(jnp.bfloat16)
        received = broadcast_dp(piece, panel_owner[p], "dp")
        term = (
            lax.dot_general(
                flat, received, (((1,), (1,)), ((), ())), preferred_element_type=jnp.float32
            )
            / cells
        )
        partials.append(reduce_scatter_slab(term, "slab"))
    gram = jnp.stack(partials, axis=1)
    return (field, gram)


def solution(mesh):
    placed = (P("dp", "slab", None), P("slab", None), P(), P())
    return jax.shard_map(
        body,
        mesh=mesh,
        in_specs=placed,
        out_specs=(P("dp", "slab", None), P(("dp", "slab"), None, None)),
        check_vma=False,
    )
```

```python
import functools

import jax
import jax.numpy as jnp
from jax import lax
from jax.experimental import pallas as pl
from jax.experimental.pallas import tpu as pltpu
from jax.sharding import PartitionSpec as P

LX = 16
PASSES = 4
PANELS = 3
PANEL = 256
HALO = 4

lateral_weight = 0.125


def broadcast_dp(piece, owner, axis):
    size = lax.axis_size(axis)
    me = lax.axis_index(axis)
    ring = size // 2
    z, oz = me // 2, owner // 2
    pair = lax.ppermute(piece, axis, [(i, i ^ 1) for i in range(size)])
    val = jnp.where(me == owner, piece, pair)
    from_below = lax.ppermute(val, axis, [(i, (i + 2) % size) for i in range(size)])
    from_above = lax.ppermute(val, axis, [(i, (i - 2) % size) for i in range(size)])
    val = jnp.where(z == oz, val, jnp.where(z == (oz + 1) % ring, from_below, from_above))
    last = lax.ppermute(val, axis, [(i, (i + 2) % size) for i in range(size)])
    return jnp.where(z == (oz + 2) % ring, last, val)


def reduce_scatter_slab(term, axis):
    size = lax.axis_size(axis)
    me = lax.axis_index(axis)
    rows = term.shape[0] // size
    part = term.reshape((size, rows) + term.shape[1:])
    bit = 1
    while bit < size:
        mine = (me // bit) % 2
        halves = part.reshape((part.shape[0] // 2, 2) + part.shape[1:])
        keep = lax.dynamic_index_in_dim(halves, mine, axis=1, keepdims=False)
        send = lax.dynamic_index_in_dim(halves, 1 - mine, axis=1, keepdims=False)
        part = keep + lax.ppermute(send, axis, [(i, i ^ bit) for i in range(size)])
        bit *= 2
    return part.reshape((rows,) + term.shape[1:])


def halo_of(shard, axis, dim):
    size, length = lax.axis_size(axis), shard.shape[dim]
    up = [(i, i + 1) for i in range(size - 1)]
    down = [(j, i) for i, j in up]
    top = lax.slice_in_dim(shard, length - HALO, length, axis=dim)
    bottom = lax.slice_in_dim(shard, 0, HALO, axis=dim)
    below = lax.ppermute(top, axis, up)
    above = lax.ppermute(bottom, axis, down)
    return jnp.concatenate([below, above], axis=dim)


def smooth_kernel(coef_ref, a_ref, h_ref, *refs, sub, aliased):
    if aliased:
        refs = refs[1:]
    o_ref, p_ref = refs
    depth, lat = a_ref.shape[1], a_ref.shape[2]
    half = lat // 2
    shape = (sub, depth, half)
    row = lax.broadcasted_iota(jnp.int32, shape, 1)
    lane = lax.broadcasted_iota(jnp.int32, shape, 2)
    low_rows, first, last = row < HALO, row == 0, row == depth - 1
    low_lanes, high_lanes = lane < LX, lane >= half - LX

    def coef(n, j, h):
        return coef_ref[n, j * depth : (j + 1) * depth, h * half : (h + 1) * half][None]

    def body(i, carry):
        r = pl.multiple_of(i * sub, sub)
        own = a_ref[pl.ds(r, sub)].astype(jnp.float32)
        hal = h_ref[pl.ds(r, sub)].astype(jnp.float32)
        own = [own[..., :half], own[..., half:]]
        hal = [hal[..., :half], hal[..., half:]]
        rot = [pltpu.roll(o, HALO, 1) for o in own]
        x = [
            [jnp.where(low_rows, hal[h], rot[h]) for h in range(2)],
            [jnp.where(low_rows, rot[h], hal[h]) for h in range(2)],
        ]
        cf = [[[coef(n, j, h) for h in range(2)] for j in range(2)] for n in range(6)]
        for _ in range(PASSES):
            depth_sum = [[None, None], [None, None]]
            for h in range(2):
                d0, d1 = pltpu.roll(x[0][h], 1, 1), pltpu.roll(x[1][h], 1, 1)
                u0, u1 = pltpu.roll(x[0][h], depth - 1, 1), pltpu.roll(x[1][h], depth - 1, 1)
                depth_sum[0][h] = d0 + jnp.where(last, u1, u0)
                depth_sum[1][h] = jnp.where(first, d0, d1) + u1
            new = [[None, None], [None, None]]
            for j in range(2):
                a, b = x[j]
                ra, rb = pltpu.roll(a, LX, 2), pltpu.roll(b, LX, 2)
                sa, sb = pltpu.roll(a, half - LX, 2), pltpu.roll(b, half - LX, 2)
                xm = [ra, jnp.where(low_lanes, ra, rb)]
                xp = [jnp.where(high_lanes, sb, sa), sb]
                for h, v in enumerate((a, b)):
                    k, cself, c_xm, c_xp, c_ym, c_yp = (cf[n][j][h] for n in range(6))
                    lateral = (
                        c_xm * xm[h]
                        + c_xp * xp[h]
                        + c_ym * pltpu.roll(v, 1, 2)
                        + c_yp * pltpu.roll(v, half - 1, 2)
                    )
                    new[j][h] = cself * v + k * depth_sum[j][h] + lateral
            x = new
        for h in range(2):
            out = jnp.where(low_rows, pltpu.roll(x[0][h], HALO, 1), pltpu.roll(x[1][h], HALO, 1))
            o_ref[pl.ds(r, sub), :, h * half : (h + 1) * half] = out
            p_ref[pl.ds(r, sub), :, h * half : (h + 1) * half] = out.astype(p_ref.dtype)
        return carry

    lax.fori_loop(0, a_ref.shape[0] // sub, body, 0)


def coefficients(kappa_col, lat):
    lane = jnp.arange(lat)[None, :]
    col = lane % LX
    k8 = lateral_weight * kappa_col
    zero = jnp.zeros_like(kappa_col)
    return jnp.stack(
        [
            kappa_col,
            1.0 - 2.0 * kappa_col - 4.0 * k8,
            jnp.where(lane >= LX, k8, zero),
            jnp.where(lane < lat - LX, k8, zero),
            jnp.where(col != 0, k8, zero),
            jnp.where(col != LX - 1, k8, zero),
        ]
    )


def smooth_chunk(field, sensitivity, halo, coef, chunk, size, block=128, sub=16):
    rows, depth, lat = sensitivity.shape
    steps = size // block
    first = chunk * steps
    aliased = field is not None
    kernel = functools.partial(smooth_kernel, sub=sub, aliased=aliased)
    in_specs = [
        pl.BlockSpec(coef.shape, lambda i: (0, 0, 0)),
        pl.BlockSpec((block, depth, lat), lambda i: (i + first, 0, 0)),
        pl.BlockSpec((block, depth, lat), lambda i: (i + first, 0, 0)),
    ]
    args = [coef, sensitivity, halo]
    if aliased:
        in_specs.append(pl.BlockSpec(memory_space=pl.ANY))
        args.append(field)
    return pl.pallas_call(
        kernel,
        grid=(steps,),
        in_specs=in_specs,
        out_specs=[
            pl.BlockSpec((block, depth, lat), lambda i: (i + first, 0, 0)),
            pl.BlockSpec((block, depth, lat), lambda i: (i, 0, 0)),
        ],
        out_shape=[
            jax.ShapeDtypeStruct((rows, depth, lat), jnp.float32),
            jax.ShapeDtypeStruct((size, depth, lat), jnp.bfloat16),
        ],
        input_output_aliases={3: 0} if aliased else {},
    )(*args)


def body(sensitivity, cell_class, class_rate, panel_owner):
    rows, depth, lat = sensitivity.shape
    onehot = (cell_class[..., None] == jnp.arange(class_rate.shape[0])[None, None, :]).astype(
        jnp.float32
    )
    kappa = jnp.sum(onehot * class_rate[None, None, :], axis=-1)
    halo = halo_of(sensitivity, "slab", 1)
    kappa_halo = halo_of(kappa, "slab", 0)
    kappa_col = jnp.concatenate([kappa_halo[:HALO], kappa, kappa_halo[HALO:]], axis=0)
    coef = coefficients(kappa_col, lat)
    field = None
    pieces = []
    for chunk in range(rows // PANEL):
        field, piece = smooth_chunk(field, sensitivity, halo, coef, chunk, PANEL)
        pieces.append(piece)
    cells = depth * lat * lax.axis_size("slab")
    flat = sensitivity.reshape(rows, depth * lat)
    partials = []
    for p in range(PANELS):
        piece = pieces[p].reshape(PANEL, depth * lat)
        received = broadcast_dp(piece, panel_owner[p], "dp")
        term = (
            lax.dot_general(
                flat, received, (((1,), (1,)), ((), ())), preferred_element_type=jnp.float32
            )
            / cells
        )
        partials.append(reduce_scatter_slab(term, "slab"))
    gram = jnp.stack(partials, axis=1)
    return (field, gram)


def solution(mesh):
    placed = (P("dp", "slab", None), P("slab", None), P(), P())
    return jax.shard_map(
        body,
        mesh=mesh,
        in_specs=placed,
        out_specs=(P("dp", "slab", None), P(("dp", "slab"), None, None)),
        check_vma=False,
    )
```

```python
import functools

import jax
import jax.numpy as jnp
from jax import lax
from jax.experimental import pallas as pl
from jax.experimental.pallas import tpu as pltpu
from jax.sharding import PartitionSpec as P

LX = 16
PASSES = 4
PANELS = 3
PANEL = 256
HALO = 4

lateral_weight = 0.125


def broadcast_dp(piece, owner, axis):
    size = lax.axis_size(axis)
    me = lax.axis_index(axis)
    ring = size // 2
    z, oz = me // 2, owner // 2
    pair = lax.ppermute(piece, axis, [(i, i ^ 1) for i in range(size)])
    val = jnp.where(me == owner, piece, pair)
    from_below = lax.ppermute(val, axis, [(i, (i + 2) % size) for i in range(size)])
    from_above = lax.ppermute(val, axis, [(i, (i - 2) % size) for i in range(size)])
    val = jnp.where(z == oz, val, jnp.where(z == (oz + 1) % ring, from_below, from_above))
    last = lax.ppermute(val, axis, [(i, (i + 2) % size) for i in range(size)])
    return jnp.where(z == (oz + 2) % ring, last, val)


def reduce_scatter_slab(term, axis):
    size = lax.axis_size(axis)
    me = lax.axis_index(axis)
    rows = term.shape[0] // size
    part = term.reshape((size, rows) + term.shape[1:])
    bit = 1
    while bit < size:
        mine = (me // bit) % 2
        halves = part.reshape((part.shape[0] // 2, 2) + part.shape[1:])
        keep = lax.dynamic_index_in_dim(halves, mine, axis=1, keepdims=False)
        send = lax.dynamic_index_in_dim(halves, 1 - mine, axis=1, keepdims=False)
        part = keep + lax.ppermute(send, axis, [(i, i ^ bit) for i in range(size)])
        bit *= 2
    return part.reshape((rows,) + term.shape[1:])


def halo_of(shard, axis, dim):
    size, length = lax.axis_size(axis), shard.shape[dim]
    up = [(i, i + 1) for i in range(size - 1)]
    down = [(j, i) for i, j in up]
    top = lax.slice_in_dim(shard, length - HALO, length, axis=dim)
    bottom = lax.slice_in_dim(shard, 0, HALO, axis=dim)
    below = lax.ppermute(top, axis, up)
    above = lax.ppermute(bottom, axis, down)
    return jnp.concatenate([below, above], axis=dim)


def smooth_kernel(coef_ref, a_ref, h_ref, *refs, sub, aliased):
    if aliased:
        refs = refs[1:]
    o_ref, p_ref = refs
    depth, lat = a_ref.shape[1], a_ref.shape[2]
    half = lat // 2
    shape = (sub, depth, half)
    row = lax.broadcasted_iota(jnp.int32, shape, 1)
    lane = lax.broadcasted_iota(jnp.int32, shape, 2)
    low_rows, first, last = row < HALO, row == 0, row == depth - 1
    low_lanes, high_lanes = lane < LX, lane >= half - LX

    def coef(n, j, h):
        return coef_ref[n, j * depth : (j + 1) * depth, h * half : (h + 1) * half][None]

    def body(i, carry):
        r = pl.multiple_of(i * sub, sub)
        own = a_ref[pl.ds(r, sub)].astype(jnp.float32)
        hal = h_ref[pl.ds(r, sub)].astype(jnp.float32)
        own = [own[..., :half], own[..., half:]]
        hal = [hal[..., :half], hal[..., half:]]
        rot = [pltpu.roll(o, HALO, 1) for o in own]
        x = [
            [jnp.where(low_rows, hal[h], rot[h]) for h in range(2)],
            [jnp.where(low_rows, rot[h], hal[h]) for h in range(2)],
        ]
        cf = [[[coef(n, j, h) for h in range(2)] for j in range(2)] for n in range(6)]
        for _ in range(PASSES):
            depth_sum = [[None, None], [None, None]]
            for h in range(2):
                d0, d1 = pltpu.roll(x[0][h], 1, 1), pltpu.roll(x[1][h], 1, 1)
                u0, u1 = pltpu.roll(x[0][h], depth - 1, 1), pltpu.roll(x[1][h], depth - 1, 1)
                depth_sum[0][h] = d0 + jnp.where(last, u1, u0)
                depth_sum[1][h] = jnp.where(first, d0, d1) + u1
            new = [[None, None], [None, None]]
            for j in range(2):
                a, b = x[j]
                ra, rb = pltpu.roll(a, LX, 2), pltpu.roll(b, LX, 2)
                sa, sb = pltpu.roll(a, half - LX, 2), pltpu.roll(b, half - LX, 2)
                xm = [ra, jnp.where(low_lanes, ra, rb)]
                xp = [jnp.where(high_lanes, sb, sa), sb]
                for h, v in enumerate((a, b)):
                    k, cself, c_xm, c_xp, c_ym, c_yp = (cf[n][j][h] for n in range(6))
                    lateral = (
                        c_xm * xm[h]
                        + c_xp * xp[h]
                        + c_ym * pltpu.roll(v, 1, 2)
                        + c_yp * pltpu.roll(v, half - 1, 2)
                    )
                    new[j][h] = cself * v + k * depth_sum[j][h] + lateral
            x = new
        for h in range(2):
            out = jnp.where(low_rows, pltpu.roll(x[0][h], HALO, 1), pltpu.roll(x[1][h], HALO, 1))
            o_ref[pl.ds(r, sub), :, h * half : (h + 1) * half] = out
            p_ref[pl.ds(r, sub), :, h * half : (h + 1) * half] = out.astype(p_ref.dtype)
        return carry

    lax.fori_loop(0, a_ref.shape[0] // sub, body, 0)


def coefficients(kappa_col, lat):
    lane = jnp.arange(lat)[None, :]
    col = lane % LX
    k8 = lateral_weight * kappa_col
    zero = jnp.zeros_like(kappa_col)
    return jnp.stack(
        [
            kappa_col,
            1.0 - 2.0 * kappa_col - 4.0 * k8,
            jnp.where(lane >= LX, k8, zero),
            jnp.where(lane < lat - LX, k8, zero),
            jnp.where(col != 0, k8, zero),
            jnp.where(col != LX - 1, k8, zero),
        ]
    )


def smooth_chunk(field, sensitivity, halo, coef, chunk, size, block=128, sub=16):
    rows, depth, lat = sensitivity.shape
    steps = size // block
    first = chunk * steps
    aliased = field is not None
    kernel = functools.partial(smooth_kernel, sub=sub, aliased=aliased)
    in_specs = [
        pl.BlockSpec(coef.shape, lambda i: (0, 0, 0)),
        pl.BlockSpec((block, depth, lat), lambda i: (i + first, 0, 0)),
        pl.BlockSpec((block, depth, lat), lambda i: (i + first, 0, 0)),
    ]
    args = [coef, sensitivity, halo]
    if aliased:
        in_specs.append(pl.BlockSpec(memory_space=pl.ANY))
        args.append(field)
    return pl.pallas_call(
        kernel,
        grid=(steps,),
        in_specs=in_specs,
        out_specs=[
            pl.BlockSpec((block, depth, lat), lambda i: (i + first, 0, 0)),
            pl.BlockSpec((block, depth, lat), lambda i: (i, 0, 0)),
        ],
        out_shape=[
            jax.ShapeDtypeStruct((rows, depth, lat), jnp.float32),
            jax.ShapeDtypeStruct((size, depth, lat), jnp.bfloat16),
        ],
        input_output_aliases={3: 0} if aliased else {},
    )(*args)


def body(sensitivity, cell_class, class_rate, panel_owner):
    rows, depth, lat = sensitivity.shape
    onehot = (cell_class[..., None] == jnp.arange(class_rate.shape[0])[None, None, :]).astype(
        jnp.float32
    )
    kappa = jnp.sum(onehot * class_rate[None, None, :], axis=-1)
    halo = halo_of(sensitivity, "slab", 1)
    kappa_halo = halo_of(kappa, "slab", 0)
    kappa_col = jnp.concatenate([kappa_halo[:HALO], kappa, kappa_halo[HALO:]], axis=0)
    coef = coefficients(kappa_col, lat)
    field = None
    pieces = []
    for chunk in range(rows // PANEL):
        field, piece = smooth_chunk(field, sensitivity, halo, coef, chunk, PANEL)
        pieces.append(piece)
    cells = depth * lat * lax.axis_size("slab")
    flat = sensitivity.reshape(rows, depth * lat)
    stacked = jnp.stack([pieces[p].reshape(PANEL, depth * lat) for p in range(PANELS)])
    owners = panel_owner[:PANELS].reshape(PANELS, 1, 1)
    received = broadcast_dp(stacked, owners, "dp").reshape(PANELS * PANEL, depth * lat)
    term = (
        lax.dot_general(flat, received, (((1,), (1,)), ((), ())), preferred_element_type=jnp.float32)
        / cells
    )
    gram = reduce_scatter_slab(term.reshape(rows, PANELS, PANEL), "slab")
    return (field, gram)


def solution(mesh):
    placed = (P("dp", "slab", None), P("slab", None), P(), P())
    return jax.shard_map(
        body,
        mesh=mesh,
        in_specs=placed,
        out_specs=(P("dp", "slab", None), P(("dp", "slab"), None, None)),
        check_vma=False,
    )
```

```python
import functools

import jax
import jax.numpy as jnp
from jax import lax
from jax.experimental import pallas as pl
from jax.experimental.pallas import tpu as pltpu
from jax.sharding import PartitionSpec as P

LX = 16
PASSES = 4
PANELS = 3
PANEL = 256
HALO = 4

lateral_weight = 0.125


def broadcast_dp(piece, owner, axis):
    size = lax.axis_size(axis)
    me = lax.axis_index(axis)
    ring = size // 2
    z, oz = me // 2, owner // 2
    pair = lax.ppermute(piece, axis, [(i, i ^ 1) for i in range(size)])
    val = jnp.where(me == owner, piece, pair)
    from_below = lax.ppermute(val, axis, [(i, (i + 2) % size) for i in range(size)])
    from_above = lax.ppermute(val, axis, [(i, (i - 2) % size) for i in range(size)])
    val = jnp.where(z == oz, val, jnp.where(z == (oz + 1) % ring, from_below, from_above))
    rows = val.shape[0] // 2
    last = jnp.concatenate(
        [
            lax.ppermute(val[:rows], axis, [(i, (i + 2) % size) for i in range(size)]),
            lax.ppermute(val[rows:], axis, [(i, (i - 2) % size) for i in range(size)]),
        ]
    )
    return jnp.where(z == (oz + 2) % ring, last, val)


def reduce_scatter_slab(term, axis):
    size = lax.axis_size(axis)
    me = lax.axis_index(axis)
    rows = term.shape[0] // size
    part = term.reshape((size, rows) + term.shape[1:])
    bit = 1
    while bit < size:
        mine = (me // bit) % 2
        halves = part.reshape((part.shape[0] // 2, 2) + part.shape[1:])
        keep = lax.dynamic_index_in_dim(halves, mine, axis=1, keepdims=False)
        send = lax.dynamic_index_in_dim(halves, 1 - mine, axis=1, keepdims=False)
        part = keep + lax.ppermute(send, axis, [(i, i ^ bit) for i in range(size)])
        bit *= 2
    return part.reshape((rows,) + term.shape[1:])


def halo_of(shard, axis, dim):
    size, length = lax.axis_size(axis), shard.shape[dim]
    up = [(i, i + 1) for i in range(size - 1)]
    down = [(j, i) for i, j in up]
    top = lax.slice_in_dim(shard, length - HALO, length, axis=dim)
    bottom = lax.slice_in_dim(shard, 0, HALO, axis=dim)
    below = lax.ppermute(top, axis, up)
    above = lax.ppermute(bottom, axis, down)
    return jnp.concatenate([below, above], axis=dim)


def smooth_kernel(coef_ref, a_ref, h_ref, o_ref, *, sub):
    depth, lat = a_ref.shape[1], a_ref.shape[2]
    half = lat // 2
    shape = (sub, depth, half)
    row = lax.broadcasted_iota(jnp.int32, shape, 1)
    lane = lax.broadcasted_iota(jnp.int32, shape, 2)
    low_rows, first, last = row < HALO, row == 0, row == depth - 1
    low_lanes, high_lanes = lane < LX, lane >= half - LX

    def coef(n, j, h):
        return coef_ref[n, j * depth : (j + 1) * depth, h * half : (h + 1) * half][None]

    def body(i, carry):
        r = pl.multiple_of(i * sub, sub)
        own = a_ref[pl.ds(r, sub)].astype(jnp.float32)
        hal = h_ref[pl.ds(r, sub)].astype(jnp.float32)
        own = [own[..., :half], own[..., half:]]
        hal = [hal[..., :half], hal[..., half:]]
        rot = [pltpu.roll(o, HALO, 1) for o in own]
        x = [
            [jnp.where(low_rows, hal[h], rot[h]) for h in range(2)],
            [jnp.where(low_rows, rot[h], hal[h]) for h in range(2)],
        ]
        cf = [[[coef(n, j, h) for h in range(2)] for j in range(2)] for n in range(6)]
        for _ in range(PASSES):
            depth_sum = [[None, None], [None, None]]
            for h in range(2):
                d0, d1 = pltpu.roll(x[0][h], 1, 1), pltpu.roll(x[1][h], 1, 1)
                u0, u1 = pltpu.roll(x[0][h], depth - 1, 1), pltpu.roll(x[1][h], depth - 1, 1)
                depth_sum[0][h] = d0 + jnp.where(last, u1, u0)
                depth_sum[1][h] = jnp.where(first, d0, d1) + u1
            new = [[None, None], [None, None]]
            for j in range(2):
                a, b = x[j]
                ra, rb = pltpu.roll(a, LX, 2), pltpu.roll(b, LX, 2)
                sa, sb = pltpu.roll(a, half - LX, 2), pltpu.roll(b, half - LX, 2)
                xm = [ra, jnp.where(low_lanes, ra, rb)]
                xp = [jnp.where(high_lanes, sb, sa), sb]
                for h, v in enumerate((a, b)):
                    k, cself, c_xm, c_xp, c_ym, c_yp = (cf[n][j][h] for n in range(6))
                    lateral = (
                        c_xm * xm[h]
                        + c_xp * xp[h]
                        + c_ym * pltpu.roll(v, 1, 2)
                        + c_yp * pltpu.roll(v, half - 1, 2)
                    )
                    new[j][h] = cself * v + k * depth_sum[j][h] + lateral
            x = new
        for h in range(2):
            out = jnp.where(low_rows, pltpu.roll(x[0][h], HALO, 1), pltpu.roll(x[1][h], HALO, 1))
            o_ref[pl.ds(r, sub), :, h * half : (h + 1) * half] = out
        return carry

    lax.fori_loop(0, a_ref.shape[0] // sub, body, 0)


def coefficients(kappa_col, lat):
    lane = jnp.arange(lat)[None, :]
    col = lane % LX
    k8 = lateral_weight * kappa_col
    zero = jnp.zeros_like(kappa_col)
    return jnp.stack(
        [
            kappa_col,
            1.0 - 2.0 * kappa_col - 4.0 * k8,
            jnp.where(lane >= LX, k8, zero),
            jnp.where(lane < lat - LX, k8, zero),
            jnp.where(col != 0, k8, zero),
            jnp.where(col != LX - 1, k8, zero),
        ]
    )


def smooth(sensitivity, halo, coef, block=128, sub=16):
    rows, depth, lat = sensitivity.shape
    kernel = functools.partial(smooth_kernel, sub=sub)
    return pl.pallas_call(
        kernel,
        grid=(rows // block,),
        in_specs=[
            pl.BlockSpec(coef.shape, lambda i: (0, 0, 0)),
            pl.BlockSpec((block, depth, lat), lambda i: (i, 0, 0)),
            pl.BlockSpec((block, depth, lat), lambda i: (i, 0, 0)),
        ],
        out_specs=pl.BlockSpec((block, depth, lat), lambda i: (i, 0, 0)),
        out_shape=jax.ShapeDtypeStruct((rows, depth, lat), jnp.float32),
    )(coef, sensitivity, halo)


def body(sensitivity, cell_class, class_rate, panel_owner):
    rows, depth, lat = sensitivity.shape
    onehot = (cell_class[..., None] == jnp.arange(class_rate.shape[0])[None, None, :]).astype(
        jnp.float32
    )
    kappa = jnp.sum(onehot * class_rate[None, None, :], axis=-1)
    halo = halo_of(sensitivity, "slab", 1)
    kappa_halo = halo_of(kappa, "slab", 0)
    kappa_col = jnp.concatenate([kappa_halo[:HALO], kappa, kappa_halo[HALO:]], axis=0)
    field = smooth(sensitivity, halo, coefficients(kappa_col, lat))
    cells = depth * lat * lax.axis_size("slab")
    flat = sensitivity.reshape(rows, depth * lat)
    partials = []
    for p in range(PANELS):
        piece = field[p * PANEL : (p + 1) * PANEL].reshape(PANEL, depth * lat).astype(jnp.bfloat16)
        received = broadcast_dp(piece, panel_owner[p], "dp")
        term = (
            lax.dot_general(
                flat, received, (((1,), (1,)), ((), ())), preferred_element_type=jnp.float32
            )
            / cells
        )
        partials.append(reduce_scatter_slab(term, "slab"))
    gram = jnp.stack(partials, axis=1)
    return (field, gram)


def solution(mesh):
    placed = (P("dp", "slab", None), P("slab", None), P(), P())
    return jax.shard_map(
        body,
        mesh=mesh,
        in_specs=placed,
        out_specs=(P("dp", "slab", None), P(("dp", "slab"), None, None)),
        check_vma=False,
    )
```

```python
import functools

import jax
import jax.numpy as jnp
from jax import lax
from jax.experimental import pallas as pl
from jax.experimental.pallas import tpu as pltpu
from jax.sharding import PartitionSpec as P

LX = 16
PASSES = 4
PANELS = 3
PANEL = 256
HALO = 4

lateral_weight = 0.125


def broadcast_dp(piece, owner, axis):
    size = lax.axis_size(axis)
    me = lax.axis_index(axis)
    ring = size // 2
    z, oz = me // 2, owner // 2
    mine = me % 2 == owner % 2
    half = piece.shape[0] // 2

    def shift(v, step):
        return lax.ppermute(v, axis, [(i, (i + step) % size) for i in range(size)])

    pair = lax.ppermute(piece[half:], axis, [(i, i ^ 1) for i in range(size)])
    val = jnp.where(mine, piece[:half], pair)
    from_below, from_above = shift(val, 2), shift(val, -2)
    val = jnp.where(z == oz, val, jnp.where(z == (oz + 1) % ring, from_below, from_above))
    quarter = half // 2
    last = jnp.concatenate([shift(val[:quarter], 2), shift(val[quarter:], -2)])
    val = jnp.where(z == (oz + 2) % ring, last, val)
    other = lax.ppermute(val, axis, [(i, i ^ 1) for i in range(size)])
    return jnp.where(mine, jnp.concatenate([val, other]), jnp.concatenate([other, val]))


def reduce_scatter_slab(term, axis):
    size = lax.axis_size(axis)
    me = lax.axis_index(axis)
    rows = term.shape[0] // size
    part = term.reshape((size, rows) + term.shape[1:])
    bit = 1
    while bit < size:
        mine = (me // bit) % 2
        halves = part.reshape((part.shape[0] // 2, 2) + part.shape[1:])
        keep = lax.dynamic_index_in_dim(halves, mine, axis=1, keepdims=False)
        send = lax.dynamic_index_in_dim(halves, 1 - mine, axis=1, keepdims=False)
        part = keep + lax.ppermute(send, axis, [(i, i ^ bit) for i in range(size)])
        bit *= 2
    return part.reshape((rows,) + term.shape[1:])


def halo_of(shard, axis, dim):
    size, length = lax.axis_size(axis), shard.shape[dim]
    up = [(i, i + 1) for i in range(size - 1)]
    down = [(j, i) for i, j in up]
    top = lax.slice_in_dim(shard, length - HALO, length, axis=dim)
    bottom = lax.slice_in_dim(shard, 0, HALO, axis=dim)
    below = lax.ppermute(top, axis, up)
    above = lax.ppermute(bottom, axis, down)
    return jnp.concatenate([below, above], axis=dim)


def smooth_kernel(coef_ref, a_ref, h_ref, o_ref, *, sub):
    depth, lat = a_ref.shape[1], a_ref.shape[2]
    half = lat // 2
    shape = (sub, depth, half)
    row = lax.broadcasted_iota(jnp.int32, shape, 1)
    lane = lax.broadcasted_iota(jnp.int32, shape, 2)
    low_rows, first, last = row < HALO, row == 0, row == depth - 1
    low_lanes, high_lanes = lane < LX, lane >= half - LX

    def coef(n, j, h):
        return coef_ref[n, j * depth : (j + 1) * depth, h * half : (h + 1) * half][None]

    def body(i, carry):
        r = pl.multiple_of(i * sub, sub)
        own = a_ref[pl.ds(r, sub)].astype(jnp.float32)
        hal = h_ref[pl.ds(r, sub)].astype(jnp.float32)
        own = [own[..., :half], own[..., half:]]
        hal = [hal[..., :half], hal[..., half:]]
        rot = [pltpu.roll(o, HALO, 1) for o in own]
        x = [
            [jnp.where(low_rows, hal[h], rot[h]) for h in range(2)],
            [jnp.where(low_rows, rot[h], hal[h]) for h in range(2)],
        ]
        cf = [[[coef(n, j, h) for h in range(2)] for j in range(2)] for n in range(6)]
        for _ in range(PASSES):
            depth_sum = [[None, None], [None, None]]
            for h in range(2):
                d0, d1 = pltpu.roll(x[0][h], 1, 1), pltpu.roll(x[1][h], 1, 1)
                u0, u1 = pltpu.roll(x[0][h], depth - 1, 1), pltpu.roll(x[1][h], depth - 1, 1)
                depth_sum[0][h] = d0 + jnp.where(last, u1, u0)
                depth_sum[1][h] = jnp.where(first, d0, d1) + u1
            new = [[None, None], [None, None]]
            for j in range(2):
                a, b = x[j]
                ra, rb = pltpu.roll(a, LX, 2), pltpu.roll(b, LX, 2)
                sa, sb = pltpu.roll(a, half - LX, 2), pltpu.roll(b, half - LX, 2)
                xm = [ra, jnp.where(low_lanes, ra, rb)]
                xp = [jnp.where(high_lanes, sb, sa), sb]
                for h, v in enumerate((a, b)):
                    k, cself, c_xm, c_xp, c_ym, c_yp = (cf[n][j][h] for n in range(6))
                    lateral = (
                        c_xm * xm[h]
                        + c_xp * xp[h]
                        + c_ym * pltpu.roll(v, 1, 2)
                        + c_yp * pltpu.roll(v, half - 1, 2)
                    )
                    new[j][h] = cself * v + k * depth_sum[j][h] + lateral
            x = new
        for h in range(2):
            out = jnp.where(low_rows, pltpu.roll(x[0][h], HALO, 1), pltpu.roll(x[1][h], HALO, 1))
            o_ref[pl.ds(r, sub), :, h * half : (h + 1) * half] = out
        return carry

    lax.fori_loop(0, a_ref.shape[0] // sub, body, 0)


def coefficients(kappa_col, lat):
    lane = jnp.arange(lat)[None, :]
    col = lane % LX
    k8 = lateral_weight * kappa_col
    zero = jnp.zeros_like(kappa_col)
    return jnp.stack(
        [
            kappa_col,
            1.0 - 2.0 * kappa_col - 4.0 * k8,
            jnp.where(lane >= LX, k8, zero),
            jnp.where(lane < lat - LX, k8, zero),
            jnp.where(col != 0, k8, zero),
            jnp.where(col != LX - 1, k8, zero),
        ]
    )


def smooth(sensitivity, halo, coef, block=128, sub=16):
    rows, depth, lat = sensitivity.shape
    kernel = functools.partial(smooth_kernel, sub=sub)
    return pl.pallas_call(
        kernel,
        grid=(rows // block,),
        in_specs=[
            pl.BlockSpec(coef.shape, lambda i: (0, 0, 0)),
            pl.BlockSpec((block, depth, lat), lambda i: (i, 0, 0)),
            pl.BlockSpec((block, depth, lat), lambda i: (i, 0, 0)),
        ],
        out_specs=pl.BlockSpec((block, depth, lat), lambda i: (i, 0, 0)),
        out_shape=jax.ShapeDtypeStruct((rows, depth, lat), jnp.float32),
    )(coef, sensitivity, halo)


def body(sensitivity, cell_class, class_rate, panel_owner):
    rows, depth, lat = sensitivity.shape
    onehot = (cell_class[..., None] == jnp.arange(class_rate.shape[0])[None, None, :]).astype(
        jnp.float32
    )
    kappa = jnp.sum(onehot * class_rate[None, None, :], axis=-1)
    halo = halo_of(sensitivity, "slab", 1)
    kappa_halo = halo_of(kappa, "slab", 0)
    kappa_col = jnp.concatenate([kappa_halo[:HALO], kappa, kappa_halo[HALO:]], axis=0)
    field = smooth(sensitivity, halo, coefficients(kappa_col, lat))
    cells = depth * lat * lax.axis_size("slab")
    flat = sensitivity.reshape(rows, depth * lat)
    partials = []
    for p in range(PANELS):
        piece = field[p * PANEL : (p + 1) * PANEL].reshape(PANEL, depth * lat).astype(jnp.bfloat16)
        received = broadcast_dp(piece, panel_owner[p], "dp")
        term = (
            lax.dot_general(
                flat, received, (((1,), (1,)), ((), ())), preferred_element_type=jnp.float32
            )
            / cells
        )
        partials.append(reduce_scatter_slab(term, "slab"))
    gram = jnp.stack(partials, axis=1)
    return (field, gram)


def solution(mesh):
    placed = (P("dp", "slab", None), P("slab", None), P(), P())
    return jax.shard_map(
        body,
        mesh=mesh,
        in_specs=placed,
        out_specs=(P("dp", "slab", None), P(("dp", "slab"), None, None)),
        check_vma=False,
    )
```

```python
import functools

import jax
import jax.numpy as jnp
from jax import lax
from jax.experimental import pallas as pl
from jax.experimental.pallas import tpu as pltpu
from jax.sharding import PartitionSpec as P

LX = 16
PASSES = 4
PANELS = 3
PANEL = 256
HALO = 4

lateral_weight = 0.125


def broadcast_dp(piece, owner, axis):
    size = lax.axis_size(axis)
    me = lax.axis_index(axis)
    ring = size // 2
    z, oz = me // 2, owner // 2
    mine = me % 2 == owner % 2
    half = piece.shape[0] // 2

    def shift(v, step):
        return lax.ppermute(v, axis, [(i, (i + step) % size) for i in range(size)])

    pair = lax.ppermute(piece[half:], axis, [(i, i ^ 1) for i in range(size)])
    val = jnp.where(mine, piece[:half], pair)
    from_below, from_above = shift(val, 2), shift(val, -2)
    val = jnp.where(z == oz, val, jnp.where(z == (oz + 1) % ring, from_below, from_above))
    quarter = half // 2
    last = jnp.concatenate([shift(val[:quarter], 2), shift(val[quarter:], -2)])
    val = jnp.where(z == (oz + 2) % ring, last, val)
    other = lax.ppermute(val, axis, [(i, i ^ 1) for i in range(size)])
    return jnp.where(mine, jnp.concatenate([val, other]), jnp.concatenate([other, val]))


def reduce_scatter_slab(term, axis):
    size = lax.axis_size(axis)
    me = lax.axis_index(axis)
    rows = term.shape[0] // size
    part = term.reshape((size, rows) + term.shape[1:])
    bit = 1
    while bit < size:
        mine = (me // bit) % 2
        halves = part.reshape((part.shape[0] // 2, 2) + part.shape[1:])
        keep = lax.dynamic_index_in_dim(halves, mine, axis=1, keepdims=False)
        send = lax.dynamic_index_in_dim(halves, 1 - mine, axis=1, keepdims=False)
        part = keep + lax.ppermute(send, axis, [(i, i ^ bit) for i in range(size)])
        bit *= 2
    return part.reshape((rows,) + term.shape[1:])


def halo_of(shard, axis, dim):
    size, length = lax.axis_size(axis), shard.shape[dim]
    up = [(i, i + 1) for i in range(size - 1)]
    down = [(j, i) for i, j in up]
    top = lax.slice_in_dim(shard, length - HALO, length, axis=dim)
    bottom = lax.slice_in_dim(shard, 0, HALO, axis=dim)
    below = lax.ppermute(top, axis, up)
    above = lax.ppermute(bottom, axis, down)
    return jnp.concatenate([below, above], axis=dim)


def smooth_kernel(coef_ref, a_ref, h_ref, *refs, sub, aliased):
    if aliased:
        refs = refs[1:]
    o_ref, p_ref = refs
    depth, lat = a_ref.shape[1], a_ref.shape[2]
    half = lat // 2
    shape = (sub, depth, half)
    row = lax.broadcasted_iota(jnp.int32, shape, 1)
    lane = lax.broadcasted_iota(jnp.int32, shape, 2)
    low_rows, first, last = row < HALO, row == 0, row == depth - 1
    low_lanes, high_lanes = lane < LX, lane >= half - LX

    def coef(n, j, h):
        return coef_ref[n, j * depth : (j + 1) * depth, h * half : (h + 1) * half][None]

    def body(i, carry):
        r = pl.multiple_of(i * sub, sub)
        own = a_ref[pl.ds(r, sub)].astype(jnp.float32)
        hal = h_ref[pl.ds(r, sub)].astype(jnp.float32)
        own = [own[..., :half], own[..., half:]]
        hal = [hal[..., :half], hal[..., half:]]
        rot = [pltpu.roll(o, HALO, 1) for o in own]
        x = [
            [jnp.where(low_rows, hal[h], rot[h]) for h in range(2)],
            [jnp.where(low_rows, rot[h], hal[h]) for h in range(2)],
        ]
        cf = [[[coef(n, j, h) for h in range(2)] for j in range(2)] for n in range(6)]
        for _ in range(PASSES):
            depth_sum = [[None, None], [None, None]]
            for h in range(2):
                d0, d1 = pltpu.roll(x[0][h], 1, 1), pltpu.roll(x[1][h], 1, 1)
                u0, u1 = pltpu.roll(x[0][h], depth - 1, 1), pltpu.roll(x[1][h], depth - 1, 1)
                depth_sum[0][h] = d0 + jnp.where(last, u1, u0)
                depth_sum[1][h] = jnp.where(first, d0, d1) + u1
            new = [[None, None], [None, None]]
            for j in range(2):
                a, b = x[j]
                ra, rb = pltpu.roll(a, LX, 2), pltpu.roll(b, LX, 2)
                sa, sb = pltpu.roll(a, half - LX, 2), pltpu.roll(b, half - LX, 2)
                xm = [ra, jnp.where(low_lanes, ra, rb)]
                xp = [jnp.where(high_lanes, sb, sa), sb]
                for h, v in enumerate((a, b)):
                    k, cself, c_xm, c_xp, c_ym, c_yp = (cf[n][j][h] for n in range(6))
                    lateral = (
                        c_xm * xm[h]
                        + c_xp * xp[h]
                        + c_ym * pltpu.roll(v, 1, 2)
                        + c_yp * pltpu.roll(v, half - 1, 2)
                    )
                    new[j][h] = cself * v + k * depth_sum[j][h] + lateral
            x = new
        for h in range(2):
            out = jnp.where(low_rows, pltpu.roll(x[0][h], HALO, 1), pltpu.roll(x[1][h], HALO, 1))
            o_ref[pl.ds(r, sub), :, h * half : (h + 1) * half] = out
            p_ref[pl.ds(r, sub), :, h * half : (h + 1) * half] = out.astype(p_ref.dtype)
        return carry

    lax.fori_loop(0, a_ref.shape[0] // sub, body, 0)


def coefficients(kappa_col, lat):
    lane = jnp.arange(lat)[None, :]
    col = lane % LX
    k8 = lateral_weight * kappa_col
    zero = jnp.zeros_like(kappa_col)
    return jnp.stack(
        [
            kappa_col,
            1.0 - 2.0 * kappa_col - 4.0 * k8,
            jnp.where(lane >= LX, k8, zero),
            jnp.where(lane < lat - LX, k8, zero),
            jnp.where(col != 0, k8, zero),
            jnp.where(col != LX - 1, k8, zero),
        ]
    )


def smooth_chunk(field, sensitivity, halo, coef, chunk, size, block=128, sub=16):
    rows, depth, lat = sensitivity.shape
    steps = size // block
    first = chunk * steps
    aliased = field is not None
    kernel = functools.partial(smooth_kernel, sub=sub, aliased=aliased)
    in_specs = [
        pl.BlockSpec(coef.shape, lambda i: (0, 0, 0)),
        pl.BlockSpec((block, depth, lat), lambda i: (i + first, 0, 0)),
        pl.BlockSpec((block, depth, lat), lambda i: (i, 0, 0)),
    ]
    args = [coef, sensitivity, halo]
    if aliased:
        in_specs.append(pl.BlockSpec(memory_space=pl.ANY))
        args.append(field)
    return pl.pallas_call(
        kernel,
        grid=(steps,),
        in_specs=in_specs,
        out_specs=[
            pl.BlockSpec((block, depth, lat), lambda i: (i + first, 0, 0)),
            pl.BlockSpec((block, depth, lat), lambda i: (i, 0, 0)),
        ],
        out_shape=[
            jax.ShapeDtypeStruct((rows, depth, lat), jnp.float32),
            jax.ShapeDtypeStruct((size, depth, lat), jnp.bfloat16),
        ],
        input_output_aliases={3: 0} if aliased else {},
    )(*args)


def body(sensitivity, cell_class, class_rate, panel_owner):
    rows, depth, lat = sensitivity.shape
    onehot = (cell_class[..., None] == jnp.arange(class_rate.shape[0])[None, None, :]).astype(
        jnp.float32
    )
    kappa = jnp.sum(onehot * class_rate[None, None, :], axis=-1)
    kappa_halo = halo_of(kappa, "slab", 0)
    kappa_col = jnp.concatenate([kappa_halo[:HALO], kappa, kappa_halo[HALO:]], axis=0)
    coef = coefficients(kappa_col, lat)
    field = None
    pieces = []
    for chunk in range(rows // PANEL):
        halo = halo_of(sensitivity[chunk * PANEL : (chunk + 1) * PANEL], "slab", 1)
        field, piece = smooth_chunk(field, sensitivity, halo, coef, chunk, PANEL)
        pieces.append(piece)
    cells = depth * lat * lax.axis_size("slab")
    flat = sensitivity.reshape(rows, depth * lat)
    partials = []
    for p in range(PANELS):
        piece = pieces[p].reshape(PANEL, depth * lat)
        received = broadcast_dp(piece, panel_owner[p], "dp")
        term = (
            lax.dot_general(
                flat, received, (((1,), (1,)), ((), ())), preferred_element_type=jnp.float32
            )
            / cells
        )
        partials.append(reduce_scatter_slab(term, "slab"))
    gram = jnp.stack(partials, axis=1)
    return (field, gram)


def solution(mesh):
    placed = (P("dp", "slab", None), P("slab", None), P(), P())
    return jax.shard_map(
        body,
        mesh=mesh,
        in_specs=placed,
        out_specs=(P("dp", "slab", None), P(("dp", "slab"), None, None)),
        check_vma=False,
    )
```

```python
import functools

import jax
import jax.numpy as jnp
from jax import lax
from jax.experimental import pallas as pl
from jax.experimental.pallas import tpu as pltpu
from jax.sharding import PartitionSpec as P

LX = 16
PASSES = 4
PANELS = 3
PANEL = 256
HALO = 4

lateral_weight = 0.125


def broadcast_dp(piece, owner, axis):
    size = lax.axis_size(axis)
    me = lax.axis_index(axis)
    ring = size // 2
    z, oz = me // 2, owner // 2
    mine = me % 2 == owner % 2
    half = piece.shape[0] // 2

    def shift(v, step):
        return lax.ppermute(v, axis, [(i, (i + step) % size) for i in range(size)])

    pair = lax.ppermute(piece[half:], axis, [(i, i ^ 1) for i in range(size)])
    val = jnp.where(mine, piece[:half], pair)
    from_below, from_above = shift(val, 2), shift(val, -2)
    val = jnp.where(z == oz, val, jnp.where(z == (oz + 1) % ring, from_below, from_above))
    quarter = half // 2
    last = jnp.concatenate([shift(val[:quarter], 2), shift(val[quarter:], -2)])
    val = jnp.where(z == (oz + 2) % ring, last, val)
    other = lax.ppermute(val, axis, [(i, i ^ 1) for i in range(size)])
    return jnp.where(mine, jnp.concatenate([val, other]), jnp.concatenate([other, val]))


def reduce_scatter_slab(term, axis):
    size = lax.axis_size(axis)
    me = lax.axis_index(axis)
    rows = term.shape[0] // size
    part = term.reshape((size, rows) + term.shape[1:])
    bit = 1
    while bit < size:
        mine = (me // bit) % 2
        halves = part.reshape((part.shape[0] // 2, 2) + part.shape[1:])
        keep = lax.dynamic_index_in_dim(halves, mine, axis=1, keepdims=False)
        send = lax.dynamic_index_in_dim(halves, 1 - mine, axis=1, keepdims=False)
        part = keep + lax.ppermute(send, axis, [(i, i ^ bit) for i in range(size)])
        bit *= 2
    return part.reshape((rows,) + term.shape[1:])


def halo_of(shard, axis, dim):
    size, length = lax.axis_size(axis), shard.shape[dim]
    up = [(i, i + 1) for i in range(size - 1)]
    down = [(j, i) for i, j in up]
    top = lax.slice_in_dim(shard, length - HALO, length, axis=dim)
    bottom = lax.slice_in_dim(shard, 0, HALO, axis=dim)
    below = lax.ppermute(top, axis, up)
    above = lax.ppermute(bottom, axis, down)
    return jnp.concatenate([below, above], axis=dim)


def smooth_kernel(coef_ref, a_ref, h_ref, o_ref, *, sub):
    depth, lat = a_ref.shape[1], a_ref.shape[2]
    half = lat // 2
    shape = (sub, depth, half)
    row = lax.broadcasted_iota(jnp.int32, shape, 1)
    lane = lax.broadcasted_iota(jnp.int32, shape, 2)
    low_rows, first, last = row < HALO, row == 0, row == depth - 1
    low_lanes, high_lanes = lane < LX, lane >= half - LX

    def coef(n, j, h):
        return coef_ref[n, j * depth : (j + 1) * depth, h * half : (h + 1) * half][None]

    def body(i, carry):
        r = pl.multiple_of(i * sub, sub)
        own = a_ref[pl.ds(r, sub)].astype(jnp.float32)
        hal = h_ref[pl.ds(r, sub)].astype(jnp.float32)
        own = [own[..., :half], own[..., half:]]
        hal = [hal[..., :half], hal[..., half:]]
        rot = [pltpu.roll(o, HALO, 1) for o in own]
        x = [
            [jnp.where(low_rows, hal[h], rot[h]) for h in range(2)],
            [jnp.where(low_rows, rot[h], hal[h]) for h in range(2)],
        ]
        cf = [[[coef(n, j, h) for h in range(2)] for j in range(2)] for n in range(6)]
        for _ in range(PASSES):
            depth_sum = [[None, None], [None, None]]
            for h in range(2):
                d0, d1 = pltpu.roll(x[0][h], 1, 1), pltpu.roll(x[1][h], 1, 1)
                u0, u1 = pltpu.roll(x[0][h], depth - 1, 1), pltpu.roll(x[1][h], depth - 1, 1)
                depth_sum[0][h] = d0 + jnp.where(last, u1, u0)
                depth_sum[1][h] = jnp.where(first, d0, d1) + u1
            new = [[None, None], [None, None]]
            for j in range(2):
                a, b = x[j]
                ra, rb = pltpu.roll(a, LX, 2), pltpu.roll(b, LX, 2)
                sa, sb = pltpu.roll(a, half - LX, 2), pltpu.roll(b, half - LX, 2)
                xm = [ra, jnp.where(low_lanes, ra, rb)]
                xp = [jnp.where(high_lanes, sb, sa), sb]
                for h, v in enumerate((a, b)):
                    k, cself, c_xm, c_xp, c_ym, c_yp = (cf[n][j][h] for n in range(6))
                    lateral = (
                        c_xm * xm[h]
                        + c_xp * xp[h]
                        + c_ym * pltpu.roll(v, 1, 2)
                        + c_yp * pltpu.roll(v, half - 1, 2)
                    )
                    new[j][h] = cself * v + k * depth_sum[j][h] + lateral
            x = new
        for h in range(2):
            out = jnp.where(low_rows, pltpu.roll(x[0][h], HALO, 1), pltpu.roll(x[1][h], HALO, 1))
            o_ref[pl.ds(r, sub), :, h * half : (h + 1) * half] = out
        return carry

    lax.fori_loop(0, a_ref.shape[0] // sub, body, 0)


def coefficients(kappa_col, lat):
    lane = jnp.arange(lat)[None, :]
    col = lane % LX
    k8 = lateral_weight * kappa_col
    zero = jnp.zeros_like(kappa_col)
    return jnp.stack(
        [
            kappa_col,
            1.0 - 2.0 * kappa_col - 4.0 * k8,
            jnp.where(lane >= LX, k8, zero),
            jnp.where(lane < lat - LX, k8, zero),
            jnp.where(col != 0, k8, zero),
            jnp.where(col != LX - 1, k8, zero),
        ]
    )


def smooth(sensitivity, halo, coef, block=128, sub=16):
    rows, depth, lat = sensitivity.shape
    kernel = functools.partial(smooth_kernel, sub=sub)
    return pl.pallas_call(
        kernel,
        grid=(rows // block,),
        in_specs=[
            pl.BlockSpec(coef.shape, lambda i: (0, 0, 0)),
            pl.BlockSpec((block, depth, lat), lambda i: (i, 0, 0)),
            pl.BlockSpec((block, depth, lat), lambda i: (i, 0, 0)),
        ],
        out_specs=pl.BlockSpec((block, depth, lat), lambda i: (i, 0, 0)),
        out_shape=jax.ShapeDtypeStruct((rows, depth, lat), jnp.float32),
    )(coef, sensitivity, halo)


def body(sensitivity, cell_class, class_rate, panel_owner):
    rows, depth, lat = sensitivity.shape
    onehot = (cell_class[..., None] == jnp.arange(class_rate.shape[0])[None, None, :]).astype(
        jnp.float32
    )
    kappa = jnp.sum(onehot * class_rate[None, None, :], axis=-1)
    halo = halo_of(sensitivity, "slab", 1)
    kappa_halo = halo_of(kappa, "slab", 0)
    kappa_col = jnp.concatenate([kappa_halo[:HALO], kappa, kappa_halo[HALO:]], axis=0)
    field = smooth(sensitivity, halo, coefficients(kappa_col, lat))
    cells = depth * lat * lax.axis_size("slab")
    flat = sensitivity.reshape(rows, depth * lat)
    partials = []
    for p in range(PANELS):
        piece = field[p * PANEL : (p + 1) * PANEL].reshape(PANEL, depth * lat).astype(jnp.bfloat16)
        received = broadcast_dp(piece, panel_owner[p], "dp")
        term = (
            lax.dot_general(
                flat, received, (((1,), (1,)), ((), ())), preferred_element_type=jnp.float32
            )
            / cells
        )
        partials.append(term)
    size = lax.axis_size("slab")
    blocks = jnp.stack(partials, axis=1).reshape(size, rows // size, PANELS, PANEL)
    gram = jnp.sum(lax.all_to_all(blocks, "slab", 0, 0, tiled=True), axis=0)
    return (field, gram)


def solution(mesh):
    placed = (P("dp", "slab", None), P("slab", None), P(), P())
    return jax.shard_map(
        body,
        mesh=mesh,
        in_specs=placed,
        out_specs=(P("dp", "slab", None), P(("dp", "slab"), None, None)),
        check_vma=False,
    )
```

```python
import functools

import jax
import jax.numpy as jnp
from jax import lax
from jax.experimental import pallas as pl
from jax.experimental.pallas import tpu as pltpu
from jax.sharding import PartitionSpec as P

LX = 16
PASSES = 4
PANELS = 3
PANEL = 256
HALO = 4

lateral_weight = 0.125


def broadcast_dp(piece, owner, axis):
    size = lax.axis_size(axis)
    me = lax.axis_index(axis)
    ring = size // 2
    z, oz = me // 2, owner // 2
    mine = me % 2 == owner % 2
    half = piece.shape[0] // 2

    def shift(v, step):
        return lax.ppermute(v, axis, [(i, (i + step) % size) for i in range(size)])

    pair = lax.ppermute(piece[half:], axis, [(i, i ^ 1) for i in range(size)])
    val = jnp.where(mine, piece[:half], pair)
    from_below, from_above = shift(val, 2), shift(val, -2)
    val = jnp.where(z == oz, val, jnp.where(z == (oz + 1) % ring, from_below, from_above))
    quarter = half // 2
    last = jnp.concatenate([shift(val[:quarter], 2), shift(val[quarter:], -2)])
    val = jnp.where(z == (oz + 2) % ring, last, val)
    other = lax.ppermute(val, axis, [(i, i ^ 1) for i in range(size)])
    return jnp.where(mine, jnp.concatenate([val, other]), jnp.concatenate([other, val]))


def reduce_scatter_slab(term, axis):
    size = lax.axis_size(axis)
    me = lax.axis_index(axis)
    rows = term.shape[0] // size
    part = term.reshape((size, rows) + term.shape[1:])
    bit = 1
    while bit < size:
        mine = (me // bit) % 2
        halves = part.reshape((part.shape[0] // 2, 2) + part.shape[1:])
        keep = lax.dynamic_index_in_dim(halves, mine, axis=1, keepdims=False)
        send = lax.dynamic_index_in_dim(halves, 1 - mine, axis=1, keepdims=False)
        part = keep + lax.ppermute(send, axis, [(i, i ^ bit) for i in range(size)])
        bit *= 2
    return part.reshape((rows,) + term.shape[1:])


def halo_of(shard, axis, dim):
    size, length = lax.axis_size(axis), shard.shape[dim]
    up = [(i, i + 1) for i in range(size - 1)]
    down = [(j, i) for i, j in up]
    top = lax.slice_in_dim(shard, length - HALO, length, axis=dim)
    bottom = lax.slice_in_dim(shard, 0, HALO, axis=dim)
    below = lax.ppermute(top, axis, up)
    above = lax.ppermute(bottom, axis, down)
    return jnp.concatenate([below, above], axis=dim)


def smooth_kernel(coef_ref, a_ref, h_ref, o_ref, p_ref, *, sub):
    depth, lat = a_ref.shape[1], a_ref.shape[2]
    half = lat // 2
    shape = (sub, depth, half)
    row = lax.broadcasted_iota(jnp.int32, shape, 1)
    lane = lax.broadcasted_iota(jnp.int32, shape, 2)
    low_rows, first, last = row < HALO, row == 0, row == depth - 1
    low_lanes, high_lanes = lane < LX, lane >= half - LX

    def coef(n, j, h):
        return coef_ref[n, j * depth : (j + 1) * depth, h * half : (h + 1) * half][None]

    def body(i, carry):
        r = pl.multiple_of(i * sub, sub)
        own = a_ref[pl.ds(r, sub)].astype(jnp.float32)
        hal = h_ref[pl.ds(r, sub)].astype(jnp.float32)
        own = [own[..., :half], own[..., half:]]
        hal = [hal[..., :half], hal[..., half:]]
        rot = [pltpu.roll(o, HALO, 1) for o in own]
        x = [
            [jnp.where(low_rows, hal[h], rot[h]) for h in range(2)],
            [jnp.where(low_rows, rot[h], hal[h]) for h in range(2)],
        ]
        cf = [[[coef(n, j, h) for h in range(2)] for j in range(2)] for n in range(6)]
        for _ in range(PASSES):
            depth_sum = [[None, None], [None, None]]
            for h in range(2):
                d0, d1 = pltpu.roll(x[0][h], 1, 1), pltpu.roll(x[1][h], 1, 1)
                u0, u1 = pltpu.roll(x[0][h], depth - 1, 1), pltpu.roll(x[1][h], depth - 1, 1)
                depth_sum[0][h] = d0 + jnp.where(last, u1, u0)
                depth_sum[1][h] = jnp.where(first, d0, d1) + u1
            new = [[None, None], [None, None]]
            for j in range(2):
                a, b = x[j]
                ra, rb = pltpu.roll(a, LX, 2), pltpu.roll(b, LX, 2)
                sa, sb = pltpu.roll(a, half - LX, 2), pltpu.roll(b, half - LX, 2)
                xm = [ra, jnp.where(low_lanes, ra, rb)]
                xp = [jnp.where(high_lanes, sb, sa), sb]
                for h, v in enumerate((a, b)):
                    k, cself, c_xm, c_xp, c_ym, c_yp = (cf[n][j][h] for n in range(6))
                    lateral = (
                        c_xm * xm[h]
                        + c_xp * xp[h]
                        + c_ym * pltpu.roll(v, 1, 2)
                        + c_yp * pltpu.roll(v, half - 1, 2)
                    )
                    new[j][h] = cself * v + k * depth_sum[j][h] + lateral
            x = new
        for h in range(2):
            out = jnp.where(low_rows, pltpu.roll(x[0][h], HALO, 1), pltpu.roll(x[1][h], HALO, 1))
            o_ref[pl.ds(r, sub), :, h * half : (h + 1) * half] = out
            p_ref[pl.ds(r, sub), :, h * half : (h + 1) * half] = out.astype(p_ref.dtype)
        return carry

    lax.fori_loop(0, a_ref.shape[0] // sub, body, 0)


def coefficients(kappa_col, lat):
    lane = jnp.arange(lat)[None, :]
    col = lane % LX
    k8 = lateral_weight * kappa_col
    zero = jnp.zeros_like(kappa_col)
    return jnp.stack(
        [
            kappa_col,
            1.0 - 2.0 * kappa_col - 4.0 * k8,
            jnp.where(lane >= LX, k8, zero),
            jnp.where(lane < lat - LX, k8, zero),
            jnp.where(col != 0, k8, zero),
            jnp.where(col != LX - 1, k8, zero),
        ]
    )


def smooth(sensitivity, halo, coef, block=128, sub=16):
    rows, depth, lat = sensitivity.shape
    kernel = functools.partial(smooth_kernel, sub=sub)
    return pl.pallas_call(
        kernel,
        grid=(rows // block,),
        in_specs=[
            pl.BlockSpec(coef.shape, lambda i: (0, 0, 0)),
            pl.BlockSpec((block, depth, lat), lambda i: (i, 0, 0)),
            pl.BlockSpec((block, depth, lat), lambda i: (i, 0, 0)),
        ],
        out_specs=[
            pl.BlockSpec((block, depth, lat), lambda i: (i, 0, 0)),
            pl.BlockSpec((block, depth, lat), lambda i: (i, 0, 0)),
        ],
        out_shape=[
            jax.ShapeDtypeStruct((rows, depth, lat), jnp.float32),
            jax.ShapeDtypeStruct((rows, depth, lat), jnp.bfloat16),
        ],
    )(coef, sensitivity, halo)


def body(sensitivity, cell_class, class_rate, panel_owner):
    rows, depth, lat = sensitivity.shape
    onehot = (cell_class[..., None] == jnp.arange(class_rate.shape[0])[None, None, :]).astype(
        jnp.float32
    )
    kappa = jnp.sum(onehot * class_rate[None, None, :], axis=-1)
    halo = halo_of(sensitivity, "slab", 1)
    kappa_halo = halo_of(kappa, "slab", 0)
    kappa_col = jnp.concatenate([kappa_halo[:HALO], kappa, kappa_halo[HALO:]], axis=0)
    field, rounded = smooth(sensitivity, halo, coefficients(kappa_col, lat))
    cells = depth * lat * lax.axis_size("slab")
    partials = []
    for p in range(PANELS):
        piece = rounded[p * PANEL : (p + 1) * PANEL]
        received = broadcast_dp(piece, panel_owner[p], "dp")
        term = (
            lax.dot_general(
                sensitivity, received, (((1, 2), (1, 2)), ((), ())), preferred_element_type=jnp.float32
            )
            / cells
        )
        partials.append(reduce_scatter_slab(term, "slab"))
    gram = jnp.stack(partials, axis=1)
    return (field, gram)


def solution(mesh):
    placed = (P("dp", "slab", None), P("slab", None), P(), P())
    return jax.shard_map(
        body,
        mesh=mesh,
        in_specs=placed,
        out_specs=(P("dp", "slab", None), P(("dp", "slab"), None, None)),
        check_vma=False,
    )
```

```python
import functools

import jax
import jax.numpy as jnp
from jax import lax
from jax.experimental import pallas as pl
from jax.experimental.pallas import tpu as pltpu
from jax.sharding import PartitionSpec as P

LX = 16
PASSES = 4
PANELS = 3
PANEL = 256
HALO = 4

lateral_weight = 0.125


def broadcast_dp(piece, owner, axis):
    size = lax.axis_size(axis)
    me = lax.axis_index(axis)
    ring = size // 2
    z, oz = me // 2, owner // 2
    mine = me % 2 == owner % 2
    half = piece.shape[0] // 2

    def shift(v, step):
        return lax.ppermute(v, axis, [(i, (i + step) % size) for i in range(size)])

    pair = lax.ppermute(piece[half:], axis, [(i, i ^ 1) for i in range(size)])
    val = jnp.where(mine, piece[:half], pair)
    from_below, from_above = shift(val, 2), shift(val, -2)
    val = jnp.where(z == oz, val, jnp.where(z == (oz + 1) % ring, from_below, from_above))
    quarter = half // 2
    last = jnp.concatenate([shift(val[:quarter], 2), shift(val[quarter:], -2)])
    val = jnp.where(z == (oz + 2) % ring, last, val)
    other = lax.ppermute(val, axis, [(i, i ^ 1) for i in range(size)])
    return jnp.where(mine, jnp.concatenate([val, other]), jnp.concatenate([other, val]))


def reduce_scatter_slab(term, axis):
    size = lax.axis_size(axis)
    me = lax.axis_index(axis)
    rows = term.shape[0] // size
    part = term.reshape((size, rows) + term.shape[1:])
    bit = 1
    while bit < size:
        mine = (me // bit) % 2
        halves = part.reshape((part.shape[0] // 2, 2) + part.shape[1:])
        keep = lax.dynamic_index_in_dim(halves, mine, axis=1, keepdims=False)
        send = lax.dynamic_index_in_dim(halves, 1 - mine, axis=1, keepdims=False)
        part = keep + lax.ppermute(send, axis, [(i, i ^ bit) for i in range(size)])
        bit *= 2
    return part.reshape((rows,) + term.shape[1:])


def halo_of(shard, axis, dim):
    size, length = lax.axis_size(axis), shard.shape[dim]
    up = [(i, i + 1) for i in range(size - 1)]
    down = [(j, i) for i, j in up]
    top = lax.slice_in_dim(shard, length - HALO, length, axis=dim)
    bottom = lax.slice_in_dim(shard, 0, HALO, axis=dim)
    below = lax.ppermute(top, axis, up)
    above = lax.ppermute(bottom, axis, down)
    return below, above


def smooth_kernel(coef_ref, a_ref, lo_ref, hi_ref, o_ref, *, sub):
    depth, lat = a_ref.shape[1], a_ref.shape[2]
    half = lat // 2
    shape = (sub, depth, half)
    row = lax.broadcasted_iota(jnp.int32, shape, 1)
    lane = lax.broadcasted_iota(jnp.int32, shape, 2)
    low_rows, first, last = row < HALO, row == 0, row == depth - 1
    low_lanes, high_lanes = lane < LX, lane >= half - LX

    def coef(n, j, h):
        return coef_ref[n, j * depth : (j + 1) * depth, h * half : (h + 1) * half][None]

    def body(i, carry):
        r = pl.multiple_of(i * sub, sub)
        own = a_ref[pl.ds(r, sub)].astype(jnp.float32)
        hal = jnp.concatenate(
            [lo_ref[pl.ds(r, sub)].astype(jnp.float32), hi_ref[pl.ds(r, sub)].astype(jnp.float32)], axis=1
        )
        own = [own[..., :half], own[..., half:]]
        hal = [hal[..., :half], hal[..., half:]]
        rot = [pltpu.roll(o, HALO, 1) for o in own]
        x = [
            [jnp.where(low_rows, hal[h], rot[h]) for h in range(2)],
            [jnp.where(low_rows, rot[h], hal[h]) for h in range(2)],
        ]
        cf = [[[coef(n, j, h) for h in range(2)] for j in range(2)] for n in range(6)]
        for _ in range(PASSES):
            depth_sum = [[None, None], [None, None]]
            for h in range(2):
                d0, d1 = pltpu.roll(x[0][h], 1, 1), pltpu.roll(x[1][h], 1, 1)
                u0, u1 = pltpu.roll(x[0][h], depth - 1, 1), pltpu.roll(x[1][h], depth - 1, 1)
                depth_sum[0][h] = d0 + jnp.where(last, u1, u0)
                depth_sum[1][h] = jnp.where(first, d0, d1) + u1
            new = [[None, None], [None, None]]
            for j in range(2):
                a, b = x[j]
                ra, rb = pltpu.roll(a, LX, 2), pltpu.roll(b, LX, 2)
                sa, sb = pltpu.roll(a, half - LX, 2), pltpu.roll(b, half - LX, 2)
                xm = [ra, jnp.where(low_lanes, ra, rb)]
                xp = [jnp.where(high_lanes, sb, sa), sb]
                for h, v in enumerate((a, b)):
                    k, cself, c_xm, c_xp, c_ym, c_yp = (cf[n][j][h] for n in range(6))
                    lateral = (
                        c_xm * xm[h]
                        + c_xp * xp[h]
                        + c_ym * pltpu.roll(v, 1, 2)
                        + c_yp * pltpu.roll(v, half - 1, 2)
                    )
                    new[j][h] = cself * v + k * depth_sum[j][h] + lateral
            x = new
        for h in range(2):
            out = jnp.where(low_rows, pltpu.roll(x[0][h], HALO, 1), pltpu.roll(x[1][h], HALO, 1))
            o_ref[pl.ds(r, sub), :, h * half : (h + 1) * half] = out
        return carry

    lax.fori_loop(0, a_ref.shape[0] // sub, body, 0)


def coefficients(kappa_col, lat):
    lane = jnp.arange(lat)[None, :]
    col = lane % LX
    k8 = lateral_weight * kappa_col
    zero = jnp.zeros_like(kappa_col)
    return jnp.stack(
        [
            kappa_col,
            1.0 - 2.0 * kappa_col - 4.0 * k8,
            jnp.where(lane >= LX, k8, zero),
            jnp.where(lane < lat - LX, k8, zero),
            jnp.where(col != 0, k8, zero),
            jnp.where(col != LX - 1, k8, zero),
        ]
    )


def smooth(sensitivity, below, above, coef, block=128, sub=16):
    rows, depth, lat = sensitivity.shape
    kernel = functools.partial(smooth_kernel, sub=sub)
    return pl.pallas_call(
        kernel,
        grid=(rows // block,),
        in_specs=[
            pl.BlockSpec(coef.shape, lambda i: (0, 0, 0)),
            pl.BlockSpec((block, depth, lat), lambda i: (i, 0, 0)),
            pl.BlockSpec((block, HALO, lat), lambda i: (i, 0, 0)),
            pl.BlockSpec((block, HALO, lat), lambda i: (i, 0, 0)),
        ],
        out_specs=pl.BlockSpec((block, depth, lat), lambda i: (i, 0, 0)),
        out_shape=jax.ShapeDtypeStruct((rows, depth, lat), jnp.float32),
    )(coef, sensitivity, below, above)


def body(sensitivity, cell_class, class_rate, panel_owner):
    rows, depth, lat = sensitivity.shape
    onehot = (cell_class[..., None] == jnp.arange(class_rate.shape[0])[None, None, :]).astype(
        jnp.float32
    )
    kappa = jnp.sum(onehot * class_rate[None, None, :], axis=-1)
    below, above = halo_of(sensitivity, "slab", 1)
    kappa_col = jnp.concatenate([halo_of(kappa, "slab", 0)[0], kappa, halo_of(kappa, "slab", 0)[1]], axis=0)
    field = smooth(sensitivity, below, above, coefficients(kappa_col, lat))
    cells = depth * lat * lax.axis_size("slab")
    flat = sensitivity.reshape(rows, depth * lat)
    partials = []
    for p in range(PANELS):
        piece = field[p * PANEL : (p + 1) * PANEL].reshape(PANEL, depth * lat).astype(jnp.bfloat16)
        received = broadcast_dp(piece, panel_owner[p], "dp")
        term = (
            lax.dot_general(
                flat, received, (((1,), (1,)), ((), ())), preferred_element_type=jnp.float32
            )
            / cells
        )
        partials.append(reduce_scatter_slab(term, "slab"))
    gram = jnp.stack(partials, axis=1)
    return (field, gram)


def solution(mesh):
    placed = (P("dp", "slab", None), P("slab", None), P(), P())
    return jax.shard_map(
        body,
        mesh=mesh,
        in_specs=placed,
        out_specs=(P("dp", "slab", None), P(("dp", "slab"), None, None)),
        check_vma=False,
    )
```

```python
import functools

import jax
import jax.numpy as jnp
from jax import lax
from jax.experimental import pallas as pl
from jax.experimental.pallas import tpu as pltpu
from jax.sharding import PartitionSpec as P

LX = 16
PASSES = 4
PANELS = 3
PANEL = 256
HALO = 4

lateral_weight = 0.125


def broadcast_dp(piece, owner, axis):
    size = lax.axis_size(axis)
    me = lax.axis_index(axis)
    ring = size // 2
    z, oz = me // 2, owner // 2
    mine = me % 2 == owner % 2
    half = piece.shape[0] // 2

    def shift(v, step):
        return lax.ppermute(v, axis, [(i, (i + step) % size) for i in range(size)])

    pair = lax.ppermute(piece[half:], axis, [(i, i ^ 1) for i in range(size)])
    val = jnp.where(mine, piece[:half], pair)
    from_below, from_above = shift(val, 2), shift(val, -2)
    val = jnp.where(z == oz, val, jnp.where(z == (oz + 1) % ring, from_below, from_above))
    quarter = half // 2
    last = jnp.concatenate([shift(val[:quarter], 2), shift(val[quarter:], -2)])
    val = jnp.where(z == (oz + 2) % ring, last, val)
    other = lax.ppermute(val, axis, [(i, i ^ 1) for i in range(size)])
    return jnp.where(mine, jnp.concatenate([val, other]), jnp.concatenate([other, val]))


def reduce_scatter_slab(term, axis):
    size = lax.axis_size(axis)
    me = lax.axis_index(axis)
    rows = term.shape[0] // size
    part = term.reshape((size, rows) + term.shape[1:])
    bit = 1
    while bit < size:
        mine = (me // bit) % 2
        halves = part.reshape((part.shape[0] // 2, 2) + part.shape[1:])
        keep = lax.dynamic_index_in_dim(halves, mine, axis=1, keepdims=False)
        send = lax.dynamic_index_in_dim(halves, 1 - mine, axis=1, keepdims=False)
        part = keep + lax.ppermute(send, axis, [(i, i ^ bit) for i in range(size)])
        bit *= 2
    return part.reshape((rows,) + term.shape[1:])


def halo_of(shard, axis, dim):
    size, length = lax.axis_size(axis), shard.shape[dim]
    up = [(i, i + 1) for i in range(size - 1)]
    down = [(j, i) for i, j in up]
    top = lax.slice_in_dim(shard, length - HALO, length, axis=dim)
    bottom = lax.slice_in_dim(shard, 0, HALO, axis=dim)
    below = lax.ppermute(top, axis, up)
    above = lax.ppermute(bottom, axis, down)
    return below, above


def smooth_kernel(coef_ref, a_ref, lo_ref, hi_ref, *refs, sub, aliased):
    o_ref = refs[-1]
    depth, lat = a_ref.shape[1], a_ref.shape[2]
    half = lat // 2
    shape = (sub, depth, half)
    row = lax.broadcasted_iota(jnp.int32, shape, 1)
    lane = lax.broadcasted_iota(jnp.int32, shape, 2)
    low_rows, first, last = row < HALO, row == 0, row == depth - 1
    low_lanes, high_lanes = lane < LX, lane >= half - LX

    def coef(n, j, h):
        return coef_ref[n, j * depth : (j + 1) * depth, h * half : (h + 1) * half][None]

    def body(i, carry):
        r = pl.multiple_of(i * sub, sub)
        own = a_ref[pl.ds(r, sub)].astype(jnp.float32)
        hal = jnp.concatenate(
            [lo_ref[pl.ds(r, sub)].astype(jnp.float32), hi_ref[pl.ds(r, sub)].astype(jnp.float32)], axis=1
        )
        own = [own[..., :half], own[..., half:]]
        hal = [hal[..., :half], hal[..., half:]]
        rot = [pltpu.roll(o, HALO, 1) for o in own]
        x = [
            [jnp.where(low_rows, hal[h], rot[h]) for h in range(2)],
            [jnp.where(low_rows, rot[h], hal[h]) for h in range(2)],
        ]
        cf = [[[coef(n, j, h) for h in range(2)] for j in range(2)] for n in range(6)]
        for _ in range(PASSES):
            depth_sum = [[None, None], [None, None]]
            for h in range(2):
                d0, d1 = pltpu.roll(x[0][h], 1, 1), pltpu.roll(x[1][h], 1, 1)
                u0, u1 = pltpu.roll(x[0][h], depth - 1, 1), pltpu.roll(x[1][h], depth - 1, 1)
                depth_sum[0][h] = d0 + jnp.where(last, u1, u0)
                depth_sum[1][h] = jnp.where(first, d0, d1) + u1
            new = [[None, None], [None, None]]
            for j in range(2):
                a, b = x[j]
                ra, rb = pltpu.roll(a, LX, 2), pltpu.roll(b, LX, 2)
                sa, sb = pltpu.roll(a, half - LX, 2), pltpu.roll(b, half - LX, 2)
                xm = [ra, jnp.where(low_lanes, ra, rb)]
                xp = [jnp.where(high_lanes, sb, sa), sb]
                for h, v in enumerate((a, b)):
                    k, cself, c_xm, c_xp, c_ym, c_yp = (cf[n][j][h] for n in range(6))
                    lateral = (
                        c_xm * xm[h]
                        + c_xp * xp[h]
                        + c_ym * pltpu.roll(v, 1, 2)
                        + c_yp * pltpu.roll(v, half - 1, 2)
                    )
                    new[j][h] = cself * v + k * depth_sum[j][h] + lateral
            x = new
        for h in range(2):
            out = jnp.where(low_rows, pltpu.roll(x[0][h], HALO, 1), pltpu.roll(x[1][h], HALO, 1))
            o_ref[pl.ds(r, sub), :, h * half : (h + 1) * half] = out
        return carry

    lax.fori_loop(0, a_ref.shape[0] // sub, body, 0)


def coefficients(kappa_col, lat):
    lane = jnp.arange(lat)[None, :]
    col = lane % LX
    k8 = lateral_weight * kappa_col
    zero = jnp.zeros_like(kappa_col)
    return jnp.stack(
        [
            kappa_col,
            1.0 - 2.0 * kappa_col - 4.0 * k8,
            jnp.where(lane >= LX, k8, zero),
            jnp.where(lane < lat - LX, k8, zero),
            jnp.where(col != 0, k8, zero),
            jnp.where(col != LX - 1, k8, zero),
        ]
    )


def smooth(sensitivity, below, above, coef, field, first, count, block=128, sub=16):
    rows, depth, lat = sensitivity.shape
    aliased = field is not None
    kernel = functools.partial(smooth_kernel, sub=sub, aliased=aliased)
    in_specs = [
        pl.BlockSpec(coef.shape, lambda i: (0, 0, 0)),
        pl.BlockSpec((block, depth, lat), lambda i: (i + first, 0, 0)),
        pl.BlockSpec((block, HALO, lat), lambda i: (i + first, 0, 0)),
        pl.BlockSpec((block, HALO, lat), lambda i: (i + first, 0, 0)),
    ]
    args = [coef, sensitivity, below, above]
    if aliased:
        in_specs.append(pl.BlockSpec(memory_space=pl.ANY))
        args.append(field)
    return pl.pallas_call(
        kernel,
        grid=(count,),
        in_specs=in_specs,
        out_specs=pl.BlockSpec((block, depth, lat), lambda i: (i + first, 0, 0)),
        out_shape=jax.ShapeDtypeStruct((rows, depth, lat), jnp.float32),
        input_output_aliases={4: 0} if aliased else {},
    )(*args)


def body(sensitivity, cell_class, class_rate, panel_owner):
    rows, depth, lat = sensitivity.shape
    onehot = (cell_class[..., None] == jnp.arange(class_rate.shape[0])[None, None, :]).astype(
        jnp.float32
    )
    kappa = jnp.sum(onehot * class_rate[None, None, :], axis=-1)
    below, above = halo_of(sensitivity, "slab", 1)
    kappa_col = jnp.concatenate([halo_of(kappa, "slab", 0)[0], kappa, halo_of(kappa, "slab", 0)[1]], axis=0)
    coef = coefficients(kappa_col, lat)
    block = 128
    head = PANELS * PANEL // block
    early = smooth(sensitivity, below, above, coef, None, 0, head, block)
    field = smooth(sensitivity, below, above, coef, early, head, rows // block - head, block)
    cells = depth * lat * lax.axis_size("slab")
    flat = sensitivity.reshape(rows, depth * lat)
    partials = []
    for p in range(PANELS):
        piece = early[p * PANEL : (p + 1) * PANEL].reshape(PANEL, depth * lat).astype(jnp.bfloat16)
        received = broadcast_dp(piece, panel_owner[p], "dp")
        term = (
            lax.dot_general(
                flat, received, (((1,), (1,)), ((), ())), preferred_element_type=jnp.float32
            )
            / cells
        )
        partials.append(reduce_scatter_slab(term, "slab"))
    gram = jnp.stack(partials, axis=1)
    return (field, gram)


def solution(mesh):
    placed = (P("dp", "slab", None), P("slab", None), P(), P())
    return jax.shard_map(
        body,
        mesh=mesh,
        in_specs=placed,
        out_specs=(P("dp", "slab", None), P(("dp", "slab"), None, None)),
        check_vma=False,
    )
```

```python
import functools

import jax
import jax.numpy as jnp
from jax import lax
from jax.experimental import pallas as pl
from jax.experimental.pallas import tpu as pltpu
from jax.sharding import PartitionSpec as P

LX = 16
PASSES = 4
PANELS = 3
PANEL = 256
HALO = 4

lateral_weight = 0.125


def broadcast_dp(piece, owner, axis):
    size = lax.axis_size(axis)
    me = lax.axis_index(axis)
    ring = size // 2
    z, oz = me // 2, owner // 2
    mine = me % 2 == owner % 2
    half = piece.shape[0] // 2

    def shift(v, step):
        return lax.ppermute(v, axis, [(i, (i + step) % size) for i in range(size)])

    pair = lax.ppermute(piece[half:], axis, [(i, i ^ 1) for i in range(size)])
    val = jnp.where(mine, piece[:half], pair)
    from_below, from_above = shift(val, 2), shift(val, -2)
    val = jnp.where(z == oz, val, jnp.where(z == (oz + 1) % ring, from_below, from_above))
    quarter = half // 2
    last = jnp.concatenate([shift(val[:quarter], 2), shift(val[quarter:], -2)])
    val = jnp.where(z == (oz + 2) % ring, last, val)
    other = lax.ppermute(val, axis, [(i, i ^ 1) for i in range(size)])
    return jnp.where(mine, jnp.concatenate([val, other]), jnp.concatenate([other, val]))


def reduce_scatter_slab(term, axis, order=(2, 4, 8, 1)):
    size = lax.axis_size(axis)
    me = lax.axis_index(axis)
    rows = term.shape[0] // size
    part = term.reshape((size, rows) + term.shape[1:])
    left = sorted(b for b in order if b < size)
    for bit in [b for b in order if b < size]:
        lo = 2 ** left.index(bit)
        mine = (me // bit) % 2
        split = part.reshape((part.shape[0] // (2 * lo), 2, lo) + part.shape[1:])
        keep = lax.dynamic_index_in_dim(split, mine, axis=1, keepdims=False)
        send = lax.dynamic_index_in_dim(split, 1 - mine, axis=1, keepdims=False)
        got = lax.ppermute(send, axis, [(i, i ^ bit) for i in range(size)])
        part = (keep + got).reshape((part.shape[0] // 2,) + part.shape[1:])
        left.remove(bit)
    return part.reshape((rows,) + term.shape[1:])


def halo_of(shard, axis, dim):
    size, length = lax.axis_size(axis), shard.shape[dim]
    up = [(i, i + 1) for i in range(size - 1)]
    down = [(j, i) for i, j in up]
    top = lax.slice_in_dim(shard, length - HALO, length, axis=dim)
    bottom = lax.slice_in_dim(shard, 0, HALO, axis=dim)
    below = lax.ppermute(top, axis, up)
    above = lax.ppermute(bottom, axis, down)
    return below, above


def smooth_kernel(coef_ref, a_ref, lo_ref, hi_ref, o_ref, *, sub):
    depth, lat = a_ref.shape[1], a_ref.shape[2]
    half = lat // 2
    shape = (sub, depth, half)
    row = lax.broadcasted_iota(jnp.int32, shape, 1)
    lane = lax.broadcasted_iota(jnp.int32, shape, 2)
    low_rows, first, last = row < HALO, row == 0, row == depth - 1
    low_lanes, high_lanes = lane < LX, lane >= half - LX

    def coef(n, j, h):
        return coef_ref[n, j * depth : (j + 1) * depth, h * half : (h + 1) * half][None]

    def body(i, carry):
        r = pl.multiple_of(i * sub, sub)
        own = a_ref[pl.ds(r, sub)].astype(jnp.float32)
        hal = jnp.concatenate(
            [lo_ref[pl.ds(r, sub)].astype(jnp.float32), hi_ref[pl.ds(r, sub)].astype(jnp.float32)], axis=1
        )
        own = [own[..., :half], own[..., half:]]
        hal = [hal[..., :half], hal[..., half:]]
        rot = [pltpu.roll(o, HALO, 1) for o in own]
        x = [
            [jnp.where(low_rows, hal[h], rot[h]) for h in range(2)],
            [jnp.where(low_rows, rot[h], hal[h]) for h in range(2)],
        ]
        cf = [[[coef(n, j, h) for h in range(2)] for j in range(2)] for n in range(6)]
        for _ in range(PASSES):
            depth_sum = [[None, None], [None, None]]
            for h in range(2):
                d0, d1 = pltpu.roll(x[0][h], 1, 1), pltpu.roll(x[1][h], 1, 1)
                u0, u1 = pltpu.roll(x[0][h], depth - 1, 1), pltpu.roll(x[1][h], depth - 1, 1)
                depth_sum[0][h] = d0 + jnp.where(last, u1, u0)
                depth_sum[1][h] = jnp.where(first, d0, d1) + u1
            new = [[None, None], [None, None]]
            for j in range(2):
                a, b = x[j]
                ra, rb = pltpu.roll(a, LX, 2), pltpu.roll(b, LX, 2)
                sa, sb = pltpu.roll(a, half - LX, 2), pltpu.roll(b, half - LX, 2)
                xm = [ra, jnp.where(low_lanes, ra, rb)]
                xp = [jnp.where(high_lanes, sb, sa), sb]
                for h, v in enumerate((a, b)):
                    k, cself, c_xm, c_xp, c_ym, c_yp = (cf[n][j][h] for n in range(6))
                    lateral = (
                        c_xm * xm[h]
                        + c_xp * xp[h]
                        + c_ym * pltpu.roll(v, 1, 2)
                        + c_yp * pltpu.roll(v, half - 1, 2)
                    )
                    new[j][h] = cself * v + k * depth_sum[j][h] + lateral
            x = new
        for h in range(2):
            out = jnp.where(low_rows, pltpu.roll(x[0][h], HALO, 1), pltpu.roll(x[1][h], HALO, 1))
            o_ref[pl.ds(r, sub), :, h * half : (h + 1) * half] = out
        return carry

    lax.fori_loop(0, a_ref.shape[0] // sub, body, 0)


def coefficients(kappa_col, lat):
    lane = jnp.arange(lat)[None, :]
    col = lane % LX
    k8 = lateral_weight * kappa_col
    zero = jnp.zeros_like(kappa_col)
    return jnp.stack(
        [
            kappa_col,
            1.0 - 2.0 * kappa_col - 4.0 * k8,
            jnp.where(lane >= LX, k8, zero),
            jnp.where(lane < lat - LX, k8, zero),
            jnp.where(col != 0, k8, zero),
            jnp.where(col != LX - 1, k8, zero),
        ]
    )


def smooth(sensitivity, below, above, coef, block=128, sub=16):
    rows, depth, lat = sensitivity.shape
    kernel = functools.partial(smooth_kernel, sub=sub)
    return pl.pallas_call(
        kernel,
        grid=(rows // block,),
        in_specs=[
            pl.BlockSpec(coef.shape, lambda i: (0, 0, 0)),
            pl.BlockSpec((block, depth, lat), lambda i: (i, 0, 0)),
            pl.BlockSpec((block, HALO, lat), lambda i: (i, 0, 0)),
            pl.BlockSpec((block, HALO, lat), lambda i: (i, 0, 0)),
        ],
        out_specs=pl.BlockSpec((block, depth, lat), lambda i: (i, 0, 0)),
        out_shape=jax.ShapeDtypeStruct((rows, depth, lat), jnp.float32),
    )(coef, sensitivity, below, above)


def body(sensitivity, cell_class, class_rate, panel_owner):
    rows, depth, lat = sensitivity.shape
    onehot = (cell_class[..., None] == jnp.arange(class_rate.shape[0])[None, None, :]).astype(
        jnp.float32
    )
    kappa = jnp.sum(onehot * class_rate[None, None, :], axis=-1)
    below, above = halo_of(sensitivity, "slab", 1)
    kappa_col = jnp.concatenate([halo_of(kappa, "slab", 0)[0], kappa, halo_of(kappa, "slab", 0)[1]], axis=0)
    field = smooth(sensitivity, below, above, coefficients(kappa_col, lat))
    cells = depth * lat * lax.axis_size("slab")
    flat = sensitivity.reshape(rows, depth * lat)
    partials = []
    for p in range(PANELS):
        piece = field[p * PANEL : (p + 1) * PANEL].reshape(PANEL, depth * lat).astype(jnp.bfloat16)
        received = broadcast_dp(piece, panel_owner[p], "dp")
        term = (
            lax.dot_general(
                flat, received, (((1,), (1,)), ((), ())), preferred_element_type=jnp.float32
            )
            / cells
        )
        partials.append(reduce_scatter_slab(term, "slab"))
    gram = jnp.stack(partials, axis=1)
    return (field, gram)


def solution(mesh):
    placed = (P("dp", "slab", None), P("slab", None), P(), P())
    return jax.shard_map(
        body,
        mesh=mesh,
        in_specs=placed,
        out_specs=(P("dp", "slab", None), P(("dp", "slab"), None, None)),
        check_vma=False,
    )
```

```python
import functools

import jax
import jax.numpy as jnp
from jax import lax
from jax.experimental import pallas as pl
from jax.experimental.pallas import tpu as pltpu
from jax.sharding import PartitionSpec as P

LX = 16
PASSES = 4
PANELS = 3
PANEL = 256
HALO = 4

lateral_weight = 0.125


def broadcast_dp(piece, owner, axis):
    size = lax.axis_size(axis)
    me = lax.axis_index(axis)
    ring = size // 2
    z, oz = me // 2, owner // 2
    mine = me % 2 == owner % 2
    half = piece.shape[0] // 2

    def shift(v, step):
        return lax.ppermute(v, axis, [(i, (i + step) % size) for i in range(size)])

    pair = lax.ppermute(piece[half:], axis, [(i, i ^ 1) for i in range(size)])
    val = jnp.where(mine, piece[:half], pair)
    from_below, from_above = shift(val, 2), shift(val, -2)
    val = jnp.where(z == oz, val, jnp.where(z == (oz + 1) % ring, from_below, from_above))
    quarter = half // 2
    last = jnp.concatenate([shift(val[:quarter], 2), shift(val[quarter:], -2)])
    val = jnp.where(z == (oz + 2) % ring, last, val)
    other = lax.ppermute(val, axis, [(i, i ^ 1) for i in range(size)])
    return jnp.where(mine, jnp.concatenate([val, other]), jnp.concatenate([other, val]))


def reduce_scatter_slab(term, axis):
    size = lax.axis_size(axis)
    me = lax.axis_index(axis)
    rows = term.shape[0] // size
    part = term.reshape((size, rows) + term.shape[1:])
    bit = 1
    while bit < size:
        mine = (me // bit) % 2
        halves = part.reshape((part.shape[0] // 2, 2) + part.shape[1:])
        keep = lax.dynamic_index_in_dim(halves, mine, axis=1, keepdims=False)
        send = lax.dynamic_index_in_dim(halves, 1 - mine, axis=1, keepdims=False)
        part = keep + lax.ppermute(send, axis, [(i, i ^ bit) for i in range(size)])
        bit *= 2
    return part.reshape((rows,) + term.shape[1:])


def halo_of(shard, axis, dim):
    size, length = lax.axis_size(axis), shard.shape[dim]
    up = [(i, i + 1) for i in range(size - 1)]
    down = [(j, i) for i, j in up]
    top = lax.slice_in_dim(shard, length - HALO, length, axis=dim)
    bottom = lax.slice_in_dim(shard, 0, HALO, axis=dim)
    below = lax.ppermute(top, axis, up)
    above = lax.ppermute(bottom, axis, down)
    return below, above


def smooth_kernel(coef_ref, a_ref, lo_ref, hi_ref, o_ref, *, sub):
    depth, lat = a_ref.shape[1], a_ref.shape[2]
    half = lat // 2
    shape = (sub, depth, half)
    row = lax.broadcasted_iota(jnp.int32, shape, 1)
    lane = lax.broadcasted_iota(jnp.int32, shape, 2)
    low_rows, first, last = row < HALO, row == 0, row == depth - 1
    low_lanes, high_lanes = lane < LX, lane >= half - LX

    def coef(n, j, h):
        return coef_ref[n, j * depth : (j + 1) * depth, h * half : (h + 1) * half][None]

    def body(i, carry):
        r = pl.multiple_of(i * sub, sub)
        own = a_ref[pl.ds(r, sub)].astype(jnp.float32)
        hal = jnp.concatenate(
            [lo_ref[pl.ds(r, sub)].astype(jnp.float32), hi_ref[pl.ds(r, sub)].astype(jnp.float32)], axis=1
        )
        own = [own[..., :half], own[..., half:]]
        hal = [hal[..., :half], hal[..., half:]]
        rot = [pltpu.roll(o, HALO, 1) for o in own]
        x = [
            [jnp.where(low_rows, hal[h], rot[h]) for h in range(2)],
            [jnp.where(low_rows, rot[h], hal[h]) for h in range(2)],
        ]
        cf = [[[coef(n, j, h) for h in range(2)] for j in range(2)] for n in range(6)]
        for _ in range(PASSES):
            depth_sum = [[None, None], [None, None]]
            for h in range(2):
                d0, d1 = pltpu.roll(x[0][h], 1, 1), pltpu.roll(x[1][h], 1, 1)
                u0, u1 = pltpu.roll(x[0][h], depth - 1, 1), pltpu.roll(x[1][h], depth - 1, 1)
                depth_sum[0][h] = d0 + jnp.where(last, u1, u0)
                depth_sum[1][h] = jnp.where(first, d0, d1) + u1
            new = [[None, None], [None, None]]
            for j in range(2):
                a, b = x[j]
                ra, rb = pltpu.roll(a, LX, 2), pltpu.roll(b, LX, 2)
                sa, sb = pltpu.roll(a, half - LX, 2), pltpu.roll(b, half - LX, 2)
                xm = [ra, jnp.where(low_lanes, ra, rb)]
                xp = [jnp.where(high_lanes, sb, sa), sb]
                for h, v in enumerate((a, b)):
                    k, cself, c_xm, c_xp, c_ym, c_yp = (cf[n][j][h] for n in range(6))
                    lateral = (
                        c_xm * xm[h]
                        + c_xp * xp[h]
                        + c_ym * pltpu.roll(v, 1, 2)
                        + c_yp * pltpu.roll(v, half - 1, 2)
                    )
                    new[j][h] = cself * v + k * depth_sum[j][h] + lateral
            x = new
        for h in range(2):
            out = jnp.where(low_rows, pltpu.roll(x[0][h], HALO, 1), pltpu.roll(x[1][h], HALO, 1))
            o_ref[pl.ds(r, sub), :, h * half : (h + 1) * half] = out
        return carry

    lax.fori_loop(0, a_ref.shape[0] // sub, body, 0)


def coefficients(kappa_col, lat):
    lane = jnp.arange(lat)[None, :]
    col = lane % LX
    k8 = lateral_weight * kappa_col
    zero = jnp.zeros_like(kappa_col)
    return jnp.stack(
        [
            kappa_col,
            1.0 - 2.0 * kappa_col - 4.0 * k8,
            jnp.where(lane >= LX, k8, zero),
            jnp.where(lane < lat - LX, k8, zero),
            jnp.where(col != 0, k8, zero),
            jnp.where(col != LX - 1, k8, zero),
        ]
    )


def smooth(sensitivity, below, above, coef, block=256, sub=16):
    rows, depth, lat = sensitivity.shape
    kernel = functools.partial(smooth_kernel, sub=sub)
    return pl.pallas_call(
        kernel,
        grid=(rows // block,),
        in_specs=[
            pl.BlockSpec(coef.shape, lambda i: (0, 0, 0)),
            pl.BlockSpec((block, depth, lat), lambda i: (i, 0, 0)),
            pl.BlockSpec((block, HALO, lat), lambda i: (i, 0, 0)),
            pl.BlockSpec((block, HALO, lat), lambda i: (i, 0, 0)),
        ],
        out_specs=pl.BlockSpec((block, depth, lat), lambda i: (i, 0, 0)),
        out_shape=jax.ShapeDtypeStruct((rows, depth, lat), jnp.float32),
    )(coef, sensitivity, below, above)


def body(sensitivity, cell_class, class_rate, panel_owner):
    rows, depth, lat = sensitivity.shape
    onehot = (cell_class[..., None] == jnp.arange(class_rate.shape[0])[None, None, :]).astype(
        jnp.float32
    )
    kappa = jnp.sum(onehot * class_rate[None, None, :], axis=-1)
    below, above = halo_of(sensitivity, "slab", 1)
    kappa_col = jnp.concatenate([halo_of(kappa, "slab", 0)[0], kappa, halo_of(kappa, "slab", 0)[1]], axis=0)
    field = smooth(sensitivity, below, above, coefficients(kappa_col, lat))
    cells = depth * lat * lax.axis_size("slab")
    flat = sensitivity.reshape(rows, depth * lat)
    partials = []
    for p in range(PANELS):
        piece = field[p * PANEL : (p + 1) * PANEL].reshape(PANEL, depth * lat).astype(jnp.bfloat16)
        received = broadcast_dp(piece, panel_owner[p], "dp")
        term = (
            lax.dot_general(
                flat, received, (((1,), (1,)), ((), ())), preferred_element_type=jnp.float32
            )
            / cells
        )
        partials.append(reduce_scatter_slab(term, "slab"))
    gram = jnp.stack(partials, axis=1)
    return (field, gram)


def solution(mesh):
    placed = (P("dp", "slab", None), P("slab", None), P(), P())
    return jax.shard_map(
        body,
        mesh=mesh,
        in_specs=placed,
        out_specs=(P("dp", "slab", None), P(("dp", "slab"), None, None)),
        check_vma=False,
    )
```

```python
import functools

import jax
import jax.numpy as jnp
from jax import lax
from jax.experimental import pallas as pl
from jax.experimental.pallas import tpu as pltpu
from jax.sharding import PartitionSpec as P

LX = 16
PASSES = 4
PANELS = 3
PANEL = 256
HALO = 4

lateral_weight = 0.125


def broadcast_dp(piece, owner, axis):
    size = lax.axis_size(axis)
    me = lax.axis_index(axis)
    ring = size // 2
    z, oz = me // 2, owner // 2
    mine = me % 2 == owner % 2
    half = piece.shape[0] // 2

    def shift(v, step):
        return lax.ppermute(v, axis, [(i, (i + step) % size) for i in range(size)])

    pair = lax.ppermute(piece[half:], axis, [(i, i ^ 1) for i in range(size)])
    val = jnp.where(mine, piece[:half], pair)
    from_below, from_above = shift(val, 2), shift(val, -2)
    val = jnp.where(z == oz, val, jnp.where(z == (oz + 1) % ring, from_below, from_above))
    quarter = half // 2
    last = jnp.concatenate([shift(val[:quarter], 2), shift(val[quarter:], -2)])
    val = jnp.where(z == (oz + 2) % ring, last, val)
    other = lax.ppermute(val, axis, [(i, i ^ 1) for i in range(size)])
    return jnp.concatenate([jnp.where(mine, val, other), jnp.where(mine, other, val)])


def reduce_scatter_slab(term, axis):
    size = lax.axis_size(axis)
    me = lax.axis_index(axis)
    rows = term.shape[0] // size
    part = term.reshape((size, rows) + term.shape[1:])
    bit = 1
    while bit < size:
        mine = (me // bit) % 2
        halves = part.reshape((part.shape[0] // 2, 2) + part.shape[1:])
        keep = lax.dynamic_index_in_dim(halves, mine, axis=1, keepdims=False)
        send = lax.dynamic_index_in_dim(halves, 1 - mine, axis=1, keepdims=False)
        part = keep + lax.ppermute(send, axis, [(i, i ^ bit) for i in range(size)])
        bit *= 2
    return part.reshape((rows,) + term.shape[1:])


def halo_of(shard, axis, dim):
    size, length = lax.axis_size(axis), shard.shape[dim]
    up = [(i, i + 1) for i in range(size - 1)]
    down = [(j, i) for i, j in up]
    top = lax.slice_in_dim(shard, length - HALO, length, axis=dim)
    bottom = lax.slice_in_dim(shard, 0, HALO, axis=dim)
    below = lax.ppermute(top, axis, up)
    above = lax.ppermute(bottom, axis, down)
    return below, above


def smooth_kernel(coef_ref, a_ref, lo_ref, hi_ref, o_ref, *, sub):
    depth, lat = a_ref.shape[1], a_ref.shape[2]
    half = lat // 2
    shape = (sub, depth, half)
    row = lax.broadcasted_iota(jnp.int32, shape, 1)
    lane = lax.broadcasted_iota(jnp.int32, shape, 2)
    low_rows, first, last = row < HALO, row == 0, row == depth - 1
    low_lanes, high_lanes = lane < LX, lane >= half - LX

    def coef(n, j, h):
        return coef_ref[n, j * depth : (j + 1) * depth, h * half : (h + 1) * half][None]

    def body(i, carry):
        r = pl.multiple_of(i * sub, sub)
        own = a_ref[pl.ds(r, sub)].astype(jnp.float32)
        hal = jnp.concatenate(
            [lo_ref[pl.ds(r, sub)].astype(jnp.float32), hi_ref[pl.ds(r, sub)].astype(jnp.float32)], axis=1
        )
        own = [own[..., :half], own[..., half:]]
        hal = [hal[..., :half], hal[..., half:]]
        rot = [pltpu.roll(o, HALO, 1) for o in own]
        x = [
            [jnp.where(low_rows, hal[h], rot[h]) for h in range(2)],
            [jnp.where(low_rows, rot[h], hal[h]) for h in range(2)],
        ]
        cf = [[[coef(n, j, h) for h in range(2)] for j in range(2)] for n in range(6)]
        for _ in range(PASSES):
            depth_sum = [[None, None], [None, None]]
            for h in range(2):
                d0, d1 = pltpu.roll(x[0][h], 1, 1), pltpu.roll(x[1][h], 1, 1)
                u0, u1 = pltpu.roll(x[0][h], depth - 1, 1), pltpu.roll(x[1][h], depth - 1, 1)
                depth_sum[0][h] = d0 + jnp.where(last, u1, u0)
                depth_sum[1][h] = jnp.where(first, d0, d1) + u1
            new = [[None, None], [None, None]]
            for j in range(2):
                a, b = x[j]
                ra, rb = pltpu.roll(a, LX, 2), pltpu.roll(b, LX, 2)
                sa, sb = pltpu.roll(a, half - LX, 2), pltpu.roll(b, half - LX, 2)
                xm = [ra, jnp.where(low_lanes, ra, rb)]
                xp = [jnp.where(high_lanes, sb, sa), sb]
                for h, v in enumerate((a, b)):
                    k, cself, c_xm, c_xp, c_ym, c_yp = (cf[n][j][h] for n in range(6))
                    lateral = (
                        c_xm * xm[h]
                        + c_xp * xp[h]
                        + c_ym * pltpu.roll(v, 1, 2)
                        + c_yp * pltpu.roll(v, half - 1, 2)
                    )
                    new[j][h] = cself * v + k * depth_sum[j][h] + lateral
            x = new
        for h in range(2):
            out = jnp.where(low_rows, pltpu.roll(x[0][h], HALO, 1), pltpu.roll(x[1][h], HALO, 1))
            o_ref[pl.ds(r, sub), :, h * half : (h + 1) * half] = out
        return carry

    lax.fori_loop(0, a_ref.shape[0] // sub, body, 0)


def coefficients(kappa_col, lat):
    lane = jnp.arange(lat)[None, :]
    col = lane % LX
    k8 = lateral_weight * kappa_col
    zero = jnp.zeros_like(kappa_col)
    return jnp.stack(
        [
            kappa_col,
            1.0 - 2.0 * kappa_col - 4.0 * k8,
            jnp.where(lane >= LX, k8, zero),
            jnp.where(lane < lat - LX, k8, zero),
            jnp.where(col != 0, k8, zero),
            jnp.where(col != LX - 1, k8, zero),
        ]
    )


def smooth(sensitivity, below, above, coef, block=128, sub=16):
    rows, depth, lat = sensitivity.shape
    kernel = functools.partial(smooth_kernel, sub=sub)
    return pl.pallas_call(
        kernel,
        grid=(rows // block,),
        in_specs=[
            pl.BlockSpec(coef.shape, lambda i: (0, 0, 0)),
            pl.BlockSpec((block, depth, lat), lambda i: (i, 0, 0)),
            pl.BlockSpec((block, HALO, lat), lambda i: (i, 0, 0)),
            pl.BlockSpec((block, HALO, lat), lambda i: (i, 0, 0)),
        ],
        out_specs=pl.BlockSpec((block, depth, lat), lambda i: (i, 0, 0)),
        out_shape=jax.ShapeDtypeStruct((rows, depth, lat), jnp.float32),
    )(coef, sensitivity, below, above)


def body(sensitivity, cell_class, class_rate, panel_owner):
    rows, depth, lat = sensitivity.shape
    onehot = (cell_class[..., None] == jnp.arange(class_rate.shape[0])[None, None, :]).astype(
        jnp.float32
    )
    kappa = jnp.sum(onehot * class_rate[None, None, :], axis=-1)
    below, above = halo_of(sensitivity, "slab", 1)
    kappa_col = jnp.concatenate([halo_of(kappa, "slab", 0)[0], kappa, halo_of(kappa, "slab", 0)[1]], axis=0)
    field = smooth(sensitivity, below, above, coefficients(kappa_col, lat))
    cells = depth * lat * lax.axis_size("slab")
    flat = sensitivity.reshape(rows, depth * lat)
    partials = []
    for p in range(PANELS):
        piece = field[p * PANEL : (p + 1) * PANEL].reshape(PANEL, depth * lat).astype(jnp.bfloat16)
        received = broadcast_dp(piece, panel_owner[p], "dp")
        term = (
            lax.dot_general(
                flat, received, (((1,), (1,)), ((), ())), preferred_element_type=jnp.float32
            )
            / cells
        )
        partials.append(reduce_scatter_slab(term, "slab"))
    gram = jnp.stack(partials, axis=1)
    return (field, gram)


def solution(mesh):
    placed = (P("dp", "slab", None), P("slab", None), P(), P())
    return jax.shard_map(
        body,
        mesh=mesh,
        in_specs=placed,
        out_specs=(P("dp", "slab", None), P(("dp", "slab"), None, None)),
        check_vma=False,
    )
```

```python
import functools

import jax
import jax.numpy as jnp
from jax import lax
from jax.experimental import pallas as pl
from jax.experimental.pallas import tpu as pltpu
from jax.sharding import PartitionSpec as P

LX = 16
PASSES = 4
PANELS = 3
PANEL = 256
HALO = 4

lateral_weight = 0.125


def broadcast_dp(piece, owner, axis):
    size = lax.axis_size(axis)
    me = lax.axis_index(axis)
    ring = size // 2
    z, oz = me // 2, owner // 2
    mine = me % 2 == owner % 2
    half = piece.shape[0] // 2

    def shift(v, step):
        return lax.ppermute(v, axis, [(i, (i + step) % size) for i in range(size)])

    pair = lax.ppermute(piece[half:], axis, [(i, i ^ 1) for i in range(size)])
    val = jnp.where(mine, piece[:half], pair)
    from_below, from_above = shift(val, 2), shift(val, -2)
    val = jnp.where(z == oz, val, jnp.where(z == (oz + 1) % ring, from_below, from_above))
    quarter = half // 2
    far = z == (oz + 2) % ring
    val = jnp.concatenate(
        [
            jnp.where(far, shift(val[:quarter], 2), val[:quarter]),
            jnp.where(far, shift(val[quarter:], -2), val[quarter:]),
        ]
    )
    other = lax.ppermute(val, axis, [(i, i ^ 1) for i in range(size)])
    return jnp.concatenate([jnp.where(mine, val, other), jnp.where(mine, other, val)])


def reduce_scatter_slab(term, axis):
    size = lax.axis_size(axis)
    me = lax.axis_index(axis)
    rows = term.shape[0] // size
    part = term.reshape((size, rows) + term.shape[1:])
    bit = 1
    while bit < size:
        mine = (me // bit) % 2
        halves = part.reshape((part.shape[0] // 2, 2) + part.shape[1:])
        keep = lax.dynamic_index_in_dim(halves, mine, axis=1, keepdims=False)
        send = lax.dynamic_index_in_dim(halves, 1 - mine, axis=1, keepdims=False)
        part = keep + lax.ppermute(send, axis, [(i, i ^ bit) for i in range(size)])
        bit *= 2
    return part.reshape((rows,) + term.shape[1:])


def halo_of(shard, axis, dim):
    size, length = lax.axis_size(axis), shard.shape[dim]
    up = [(i, i + 1) for i in range(size - 1)]
    down = [(j, i) for i, j in up]
    top = lax.slice_in_dim(shard, length - HALO, length, axis=dim)
    bottom = lax.slice_in_dim(shard, 0, HALO, axis=dim)
    below = lax.ppermute(top, axis, up)
    above = lax.ppermute(bottom, axis, down)
    return below, above


def smooth_kernel(coef_ref, a_ref, lo_ref, hi_ref, o_ref, *, sub):
    depth, lat = a_ref.shape[1], a_ref.shape[2]
    half = lat // 2
    shape = (sub, depth, half)
    row = lax.broadcasted_iota(jnp.int32, shape, 1)
    lane = lax.broadcasted_iota(jnp.int32, shape, 2)
    low_rows, first, last = row < HALO, row == 0, row == depth - 1
    low_lanes, high_lanes = lane < LX, lane >= half - LX

    def coef(n, j, h):
        return coef_ref[n, j * depth : (j + 1) * depth, h * half : (h + 1) * half][None]

    def body(i, carry):
        r = pl.multiple_of(i * sub, sub)
        own = a_ref[pl.ds(r, sub)].astype(jnp.float32)
        hal = jnp.concatenate(
            [lo_ref[pl.ds(r, sub)].astype(jnp.float32), hi_ref[pl.ds(r, sub)].astype(jnp.float32)], axis=1
        )
        own = [own[..., :half], own[..., half:]]
        hal = [hal[..., :half], hal[..., half:]]
        rot = [pltpu.roll(o, HALO, 1) for o in own]
        x = [
            [jnp.where(low_rows, hal[h], rot[h]) for h in range(2)],
            [jnp.where(low_rows, rot[h], hal[h]) for h in range(2)],
        ]
        cf = [[[coef(n, j, h) for h in range(2)] for j in range(2)] for n in range(6)]
        for _ in range(PASSES):
            depth_sum = [[None, None], [None, None]]
            for h in range(2):
                d0, d1 = pltpu.roll(x[0][h], 1, 1), pltpu.roll(x[1][h], 1, 1)
                u0, u1 = pltpu.roll(x[0][h], depth - 1, 1), pltpu.roll(x[1][h], depth - 1, 1)
                depth_sum[0][h] = d0 + jnp.where(last, u1, u0)
                depth_sum[1][h] = jnp.where(first, d0, d1) + u1
            new = [[None, None], [None, None]]
            for j in range(2):
                a, b = x[j]
                ra, rb = pltpu.roll(a, LX, 2), pltpu.roll(b, LX, 2)
                sa, sb = pltpu.roll(a, half - LX, 2), pltpu.roll(b, half - LX, 2)
                xm = [ra, jnp.where(low_lanes, ra, rb)]
                xp = [jnp.where(high_lanes, sb, sa), sb]
                for h, v in enumerate((a, b)):
                    k, cself, c_xm, c_xp, c_ym, c_yp = (cf[n][j][h] for n in range(6))
                    lateral = (
                        c_xm * xm[h]
                        + c_xp * xp[h]
                        + c_ym * pltpu.roll(v, 1, 2)
                        + c_yp * pltpu.roll(v, half - 1, 2)
                    )
                    new[j][h] = cself * v + k * depth_sum[j][h] + lateral
            x = new
        for h in range(2):
            out = jnp.where(low_rows, pltpu.roll(x[0][h], HALO, 1), pltpu.roll(x[1][h], HALO, 1))
            o_ref[pl.ds(r, sub), :, h * half : (h + 1) * half] = out
        return carry

    lax.fori_loop(0, a_ref.shape[0] // sub, body, 0)


def coefficients(kappa_col, lat):
    lane = jnp.arange(lat)[None, :]
    col = lane % LX
    k8 = lateral_weight * kappa_col
    zero = jnp.zeros_like(kappa_col)
    return jnp.stack(
        [
            kappa_col,
            1.0 - 2.0 * kappa_col - 4.0 * k8,
            jnp.where(lane >= LX, k8, zero),
            jnp.where(lane < lat - LX, k8, zero),
            jnp.where(col != 0, k8, zero),
            jnp.where(col != LX - 1, k8, zero),
        ]
    )


def smooth(sensitivity, below, above, coef, block=128, sub=16):
    rows, depth, lat = sensitivity.shape
    kernel = functools.partial(smooth_kernel, sub=sub)
    return pl.pallas_call(
        kernel,
        grid=(rows // block,),
        in_specs=[
            pl.BlockSpec(coef.shape, lambda i: (0, 0, 0)),
            pl.BlockSpec((block, depth, lat), lambda i: (i, 0, 0)),
            pl.BlockSpec((block, HALO, lat), lambda i: (i, 0, 0)),
            pl.BlockSpec((block, HALO, lat), lambda i: (i, 0, 0)),
        ],
        out_specs=pl.BlockSpec((block, depth, lat), lambda i: (i, 0, 0)),
        out_shape=jax.ShapeDtypeStruct((rows, depth, lat), jnp.float32),
    )(coef, sensitivity, below, above)


def body(sensitivity, cell_class, class_rate, panel_owner):
    rows, depth, lat = sensitivity.shape
    onehot = (cell_class[..., None] == jnp.arange(class_rate.shape[0])[None, None, :]).astype(
        jnp.float32
    )
    kappa = jnp.sum(onehot * class_rate[None, None, :], axis=-1)
    below, above = halo_of(sensitivity, "slab", 1)
    kappa_col = jnp.concatenate([halo_of(kappa, "slab", 0)[0], kappa, halo_of(kappa, "slab", 0)[1]], axis=0)
    field = smooth(sensitivity, below, above, coefficients(kappa_col, lat))
    cells = depth * lat * lax.axis_size("slab")
    flat = sensitivity.reshape(rows, depth * lat)
    partials = []
    for p in range(PANELS):
        piece = field[p * PANEL : (p + 1) * PANEL].reshape(PANEL, depth * lat).astype(jnp.bfloat16)
        received = broadcast_dp(piece, panel_owner[p], "dp")
        term = (
            lax.dot_general(
                flat, received, (((1,), (1,)), ((), ())), preferred_element_type=jnp.float32
            )
            / cells
        )
        partials.append(reduce_scatter_slab(term, "slab"))
    gram = jnp.stack(partials, axis=1)
    return (field, gram)


def solution(mesh):
    placed = (P("dp", "slab", None), P("slab", None), P(), P())
    return jax.shard_map(
        body,
        mesh=mesh,
        in_specs=placed,
        out_specs=(P("dp", "slab", None), P(("dp", "slab"), None, None)),
        check_vma=False,
    )
```
